256 devices in a mesh: gx: 64 (over x, y, z_hi, core), gy: 4 (over z_lo).
Axes of the slice: x: 4, y: 4, z: 8 (z_hi: 2, z_lo: 4; z = z_hi * 4 + z_lo), core: 2. Of those that a mesh axis runs over, the one named last changes fastest.
Arguments:
- features: bfloat16 [64, 4, 2, 8, 8, 8, 128], P('gx', 'gy'), may hold values from -6 to 6
- cotangent: bfloat16 [64, 4, 2, 4, 4, 4, 256], P('gx', 'gy'), may hold values from -6 to 6
- conv_first: bfloat16 [27, 128, 128], replicated, may hold values from -0.109375 to 0.109375
- down_weight: bfloat16 [8, 128, 256], replicated, may hold values from -0.1875 to 0.1875
- conv_second: bfloat16 [27, 256, 256], replicated, may hold values from -0.078125 to 0.078125
- block_count: int32 [64, 4], P('gx', 'gy'), may hold values from 1 to 2, as said below
- neighbours: int32 [64, 4, 2, 26], P('gx', 'gy'), may hold values from -1 to 1, as said below
Outputs:
- output_field: bfloat16 [64, 4, 2, 4, 4, 4, 256], P('gx', 'gy')
- input_grad: bfloat16 [64, 4, 2, 8, 8, 8, 128], P('gx', 'gy')
- grad_first: float32 [27, 128, 128], P(None, 'gx')
- grad_down: float32 [8, 128, 256], P(None, 'gx')
- grad_second: float32 [27, 256, 256], P(None, 'gx')
The draws below stay inside these ranges and needn't reach their ends.
Inputs may be any that keep to these rules, and one draw needn't show every extreme that they name: `block_count`: each column holds 1 to 2 active blocks at distinct levels of its 8, in slots 0 up to its count in rising level; some column holds exactly 2. neighbours[i, j, s, k] is the slot, in column (i + ox, j + oy), of the active block oz levels from slot s's block, for the k-th nonzero offset (ox, oy, oz) with ox slowest and oz fastest, or -1 where there is none; it is below that column's count; rows of slots at or past block_count[i, j] are all -1; the relation is symmetric.
All inputs are finite; a program needn't handle non-finite values.
Results may differ from the reference program's by a relative error of at most 0.01.
Values may be sent and summed in bfloat16 or wider, within the bound.
No kernel may reach another device: no remote copies, remote signals or barrier semaphores. Data moves between devices by JAX's collectives and lax.ppermute only.
A program may use at most 128 MiB of HBM per device.

```python
import math
import jax
import jax.numpy as jnp
from jax import lax

C1 = 128
C2 = 256
VOX = 8
HALF = 4
LEVELS = 8
CAP = 2
COLS_X = 64
COLS_Y = 4


def geometry(key):
    geometry_key = jax.random.fold_in(key, 11)
    count_key, pick_key, level_key = jax.random.split(geometry_key, 3)
    dice_rolls = jax.random.randint(count_key, (COLS_X, COLS_Y), 0, 8)
    counts = jnp.maximum(1, CAP * (dice_rolls - 3) // 4).reshape(-1)
    busiest = jax.random.randint(pick_key, (), 0, COLS_X * COLS_Y)
    counts = jnp.where(jnp.arange(COLS_X * COLS_Y) == busiest, CAP, counts).reshape(COLS_X, COLS_Y).astype(jnp.int32)
    scores = jax.random.randint(level_key, (COLS_X, COLS_Y, LEVELS), 0, 1 << 20) * LEVELS + jnp.arange(LEVELS)
    level_rank = jnp.argsort(jnp.argsort(scores, axis=-1), axis=-1)
    occupied = level_rank < counts[..., None]
    slot_of_level = jnp.where(occupied, jnp.cumsum(occupied.astype(jnp.int32), axis=-1) - 1, -1)
    matches = slot_of_level[:, :, None, :] == jnp.arange(CAP)[None, None, :, None]
    level_of_slot = jnp.sum(jnp.where(matches, jnp.arange(LEVELS)[None, None, None, :], 0), axis=-1)
    live_slots = jnp.any(matches, axis=-1)
    padded = jnp.pad(slot_of_level, ((1, 1), (1, 1), (1, 1)), constant_values=-1)
    columns = []
    for offset_x in (-1, 0, 1):
        for offset_y in (-1, 0, 1):
            for offset_z in (-1, 0, 1):
                if offset_x == 0 and offset_y == 0 and (offset_z == 0):
                    continue
                shifted = padded[1 + offset_x:1 + offset_x + COLS_X, 1 + offset_y:1 + offset_y + COLS_Y, :]
                level_index = (level_of_slot + 1 + offset_z).astype(jnp.int32)
                neighbour_slot = jnp.take_along_axis(shifted, level_index, axis=-1)
                columns.append(jnp.where(live_slots, neighbour_slot, -1))
    return (counts, jnp.stack(columns, axis=-1).astype(jnp.int32))


def draw_block_count(key, part):
    return geometry(key)[0]


def draw_neighbours(key, part):
    return geometry(key)[1]


def shard_levels(rng, shape, cuts, least, largest):
    def one(dim, shards_of):
        draws = jax.random.uniform(jax.random.fold_in(jax.random.fold_in(rng, 6), dim), (shards_of,), jnp.float32, least / len(cuts), largest / len(cuts))
        return jnp.repeat(jnp.exp(draws), shape[dim] // shards_of).reshape((-1,) + (1,) * (len(shape) - dim - 1))

    loudness = one(*cuts[0])
    for cut in cuts[1:]:
        loudness = loudness * one(*cut)
    return loudness


def bell_draw(own_key, shape, scale, bound, cuts=(), kind=jnp.bfloat16):
    entries = scale * jax.random.normal(own_key, shape, jnp.float32)
    if cuts:
        entries = entries * shard_levels(own_key, shape, cuts, -0.22, 0.18)
    return jnp.clip(entries, -bound, bound).astype(kind)


def setup_inputs(seed: int = 0) -> dict:
    key_list = jax.random.split(jax.random.key(seed), 8)
    return {
        "features": bell_draw(key_list[0], (COLS_X, COLS_Y, CAP, VOX, VOX, VOX, C1), 1.0, 6.0, ((0, 64), (1, 4))),
        "cotangent": bell_draw(key_list[1], (COLS_X, COLS_Y, CAP, HALF, HALF, HALF, C2), 1.0, 6.0, ((0, 64), (1, 4))),
        "conv_first": bell_draw(key_list[2], (27, C1, C1), (27 * C1) ** -0.5, 0.109375),
        "down_weight": bell_draw(key_list[3], (8, C1, C2), (8 * C1) ** -0.5, 0.1875),
        "conv_second": bell_draw(key_list[4], (27, C2, C2), (27 * C2) ** -0.5, 0.078125),
        "block_count": draw_block_count(jax.random.fold_in(key_list[7], 71), 0),
        "neighbours": draw_neighbours(jax.random.fold_in(key_list[7], 71), 0),
    }


NEIGHBOUR_STEPS = (-1, 0, 1)

def column_of(offset_x, offset_y, offset_z):
    raster = 9 * (offset_x + 1) + 3 * (offset_y + 1) + (offset_z + 1)
    return raster - 1 if raster > 13 else raster

def outer_layer(values, axis, border):
    length = values.shape[axis]
    first_index = 0 if border == 0 else length - 1
    return lax.slice_in_dim(values, first_index, first_index + 1, axis=axis)

def shift_devices(values, axis, stride):
    length = values.shape[axis]
    blank_layer = jnp.zeros_like(lax.slice_in_dim(values, 0, 1, axis=axis))
    if stride == 1:
        return jnp.concatenate([blank_layer, lax.slice_in_dim(values, 0, length - 1, axis=axis)], axis=axis)
    return jnp.concatenate([lax.slice_in_dim(values, 1, length, axis=axis), blank_layer], axis=axis)

def device_faces(volume):
    nearby = {}
    onward = {}
    for stride in (1, -1):
        border = 1 if stride == 1 else 0
        planar = outer_layer(volume, 3, border)
        nearby[-stride, 0] = shift_devices(planar, 0, stride)
        onward[-stride, 0] = shift_devices(outer_layer(planar, 4, 0), 0, stride)
        onward[-stride, 1] = shift_devices(outer_layer(planar, 4, 1), 0, stride)
    for stride in (1, -1):
        border = 1 if stride == 1 else 0
        nearby[0, -stride] = shift_devices(outer_layer(volume, 4, border), 1, stride)
        nearby[-1, -stride] = shift_devices(onward[-1, border], 1, stride)
        nearby[1, -stride] = shift_devices(onward[1, border], 1, stride)
    return {offset: portion.reshape((-1,) + portion.shape[2:]) for offset, portion in nearby.items()}

def surround(center, nearby, slot_table):
    depth = center.shape[3]
    slabs_x = []
    for offset_x in NEIGHBOUR_STEPS:
        slabs_y = []
        for offset_y in NEIGHBOUR_STEPS:
            source = center if offset_x == 0 and offset_y == 0 else nearby[offset_x, offset_y]
            pieces = []
            for offset_z in NEIGHBOUR_STEPS:
                if offset_x == 0 and offset_y == 0 and (offset_z == 0):
                    pieces.append(center)
                else:
                    slot_ids = slot_table[:, column_of(offset_x, offset_y, offset_z)]
                    picked = jnp.take(source, jnp.maximum(slot_ids, 0), axis=0)
                    picked = jnp.where((slot_ids >= 0)[:, None, None, None, None], picked, jnp.zeros((), picked.dtype))
                    if offset_z == -1:
                        picked = picked[:, :, :, depth - 1:]
                    elif offset_z == 1:
                        picked = picked[:, :, :, :1]
                    pieces.append(picked)
            slabs_y.append(jnp.concatenate(pieces, axis=3))
        slabs_x.append(jnp.concatenate(slabs_y, axis=2))
    return jnp.concatenate(slabs_x, axis=1)

def unfold(padded, extent):
    windows = []
    for along_x in range(3):
        for along_y in range(3):
            for along_z in range(3):
                windows.append(padded[:, along_x:along_x + extent, along_y:along_y + extent, along_z:along_z + extent, :])
    stacked = jnp.concatenate(windows, axis=-1)
    return stacked.reshape(-1, stacked.shape[-1])

def into_cells(blocks, half_edge):
    slot_count, channels = (blocks.shape[0], blocks.shape[-1])
    lattice = blocks.reshape(slot_count, half_edge, 2, half_edge, 2, half_edge, 2, channels)
    lattice = lattice.transpose(0, 1, 3, 5, 2, 4, 6, 7)
    return lattice.reshape(slot_count * half_edge ** 3, 8 * channels)

def from_cells(cell_rows, slot_count, half_edge, channels):
    lattice = cell_rows.reshape(slot_count, half_edge, half_edge, half_edge, 2, 2, 2, channels)
    lattice = lattice.transpose(0, 1, 4, 2, 5, 3, 6, 7)
    return lattice.reshape(slot_count, 2 * half_edge, 2 * half_edge, 2 * half_edge, channels)

def silu_slope(values):
    logistic = jax.nn.sigmoid(values)
    return logistic * (1.0 + values * (1.0 - logistic))

def contract_rows(left, right):
    return lax.dot_general(left, right, (((0,), (0,)), ((), ())), preferred_element_type=jnp.float32)

def reference(features, cotangent, conv_first, down_weight, conv_second, block_count, neighbours):
    devices = COLS_X * COLS_Y
    live_slots = jnp.arange(CAP)[None, None, :] < block_count[:, :, None]
    live_mask = live_slots[..., None, None, None, None]
    inputs = jnp.where(live_mask, features, jnp.zeros((), features.dtype))
    seed_blocks = jnp.where(live_mask, cotangent, jnp.zeros((), cotangent.dtype))
    tables = neighbours.reshape(devices, CAP, 26)
    flat_inputs = inputs.reshape((devices,) + inputs.shape[2:])
    flat_seeds = seed_blocks.reshape((devices,) + seed_blocks.shape[2:])
    first_matrix = conv_first.reshape(-1, C1)
    down_matrix = down_weight.reshape(-1, C2)
    second_matrix = conv_second.reshape(-1, C2)
    first_flip = jnp.transpose(conv_first[::-1], (0, 2, 1)).reshape(-1, C1)
    second_flip = jnp.transpose(conv_second[::-1], (0, 2, 1)).reshape(-1, C2)
    near_input = device_faces(inputs)

    def first_forward(packed):
        center, nearby, slot_table = packed
        return jnp.dot(unfold(surround(center, nearby, slot_table), VOX), first_matrix, preferred_element_type=jnp.float32)
    pre_first = lax.map(first_forward, (flat_inputs, near_input, tables))
    hidden_first = jax.nn.silu(pre_first).astype(jnp.bfloat16)
    first_cells = lax.map(lambda hidden: into_cells(hidden.reshape(CAP, VOX, VOX, VOX, C1), HALF), hidden_first)
    cell_matrix = first_cells.reshape(-1, 8 * C1)
    pre_down = jnp.dot(cell_matrix, down_matrix, preferred_element_type=jnp.float32)
    hidden_down = jax.nn.silu(pre_down).astype(jnp.bfloat16).reshape(devices, CAP, HALF, HALF, HALF, C2)
    near_hidden = device_faces(hidden_down.reshape(COLS_X, COLS_Y, CAP, HALF, HALF, HALF, C2))

    def second_forward(packed):
        center, nearby, slot_table = packed
        return jnp.dot(unfold(surround(center, nearby, slot_table), HALF), second_matrix, preferred_element_type=jnp.float32)
    output_field = lax.map(second_forward, (hidden_down, near_hidden, tables)).astype(jnp.bfloat16)
    near_seed = device_faces(seed_blocks)

    def second_back(packed):
        center, nearby, slot_table = packed
        return jnp.dot(unfold(surround(center, nearby, slot_table), HALF), second_flip, preferred_element_type=jnp.float32)
    back_down = lax.map(second_back, (flat_seeds, near_seed, tables)).reshape(-1, C2)
    delta_down = (back_down * silu_slope(pre_down)).astype(jnp.bfloat16)

    def second_grad(total, packed):
        center, nearby, slot_table, seed_rows = packed
        columns = unfold(surround(center, nearby, slot_table), HALF)
        return (total + contract_rows(columns, seed_rows.reshape(-1, C2)), None)
    grad_second, _ = lax.scan(second_grad, jnp.zeros((27 * C2, C2), jnp.float32), (hidden_down, near_hidden, tables, flat_seeds))
    grad_down = contract_rows(cell_matrix, delta_down)
    back_cells = lax.dot_general(delta_down, down_matrix, (((1,), (1,)), ((), ())), preferred_element_type=jnp.float32)
    back_cells = back_cells.reshape(devices, CAP * HALF ** 3, 8 * C1)
    back_first = lax.map(lambda cell_rows: from_cells(cell_rows, CAP, HALF, C1).reshape(-1, C1), back_cells)
    delta_first = (back_first * silu_slope(pre_first)).astype(jnp.bfloat16)
    delta_blocks = delta_first.reshape(COLS_X, COLS_Y, CAP, VOX, VOX, VOX, C1)
    near_delta = device_faces(delta_blocks)

    def first_back(packed):
        center, nearby, slot_table = packed
        return jnp.dot(unfold(surround(center, nearby, slot_table), VOX), first_flip, preferred_element_type=jnp.float32)
    input_grad = lax.map(first_back, (delta_first.reshape(devices, CAP, VOX, VOX, VOX, C1), near_delta, tables)).astype(jnp.bfloat16)

    def first_grad(total, packed):
        center, nearby, slot_table, delta_rows = packed
        columns = unfold(surround(center, nearby, slot_table), VOX)
        return (total + contract_rows(columns, delta_rows), None)
    grad_first, _ = lax.scan(first_grad, jnp.zeros((27 * C1, C1), jnp.float32), (flat_inputs, near_input, tables, delta_first))
    scale_first = 1.0 / math.sqrt(float(devices * CAP * VOX ** 3))
    scale_half = 1.0 / math.sqrt(float(devices * CAP * HALF ** 3))
    return (output_field.reshape(COLS_X, COLS_Y, CAP, HALF, HALF, HALF, C2), input_grad.reshape(COLS_X, COLS_Y, CAP, VOX, VOX, VOX, C1), grad_first.reshape(27, C1, C1) * scale_first, grad_down.reshape(8, C1, C2) * scale_half, grad_second.reshape(27, C2, C2) * scale_half)
```

```python
import math

import jax
import jax.numpy as jnp
import numpy as np
from jax import lax
from jax.sharding import PartitionSpec as P


def shifted(block, axis, distance):
    devices = range(lax.axis_size(axis))
    route = [(i - distance, i) for i in devices if i - distance in devices]
    return lax.ppermute(block, axis, route)


def send_packed(pieces, axis, distance):
    flat = jnp.concatenate([piece.reshape(-1) for piece in pieces])
    arrived = shifted(flat, axis, distance)
    out, start = [], 0
    for piece in pieces:
        out.append(arrived[start : start + piece.size].reshape(piece.shape))
        start += piece.size
    return out


def extend_xy(fields):
    depth = [f.shape[1] for f in fields]
    from_left = send_packed([f[:, e - 1 : e] for f, e in zip(fields, depth)], "gx", 1)
    from_right = send_packed([f[:, 0:1] for f in fields], "gx", -1)
    wide = [jnp.concatenate([l, f, r], axis=1) for l, f, r in zip(from_left, fields, from_right)]
    from_down = send_packed([w[:, :, e - 1 : e] for w, e in zip(wide, depth)], "gy", 1)
    from_up = send_packed([w[:, :, 0:1] for w in wide], "gy", -1)
    return [jnp.concatenate([d, w, u], axis=2) for d, w, u in zip(from_down, wide, from_up)]


def source_table(slot_table, extent):
    slot_count = slot_table.shape[0]
    own = jnp.arange(slot_count, dtype=slot_table.dtype)[:, None]
    full = jnp.concatenate([slot_table[:, :13], own, slot_table[:, 13:]], axis=1)
    full = full.reshape(slot_count, 3, 3, 3)
    reps = np.array([1, extent, 1])
    for axis in (1, 2, 3):
        full = jnp.repeat(full, reps, axis=axis, total_repeat_length=extent + 2)
    return full


def pad_field(wide, sources):
    extent = wide.shape[3]
    tall = jnp.concatenate([wide[:, :, :, extent - 1 :], wide, wide[:, :, :, :1]], axis=3)
    padded = jnp.zeros((sources.shape[0],) + tall.shape[1:], tall.dtype)
    for slot in range(tall.shape[0]):
        padded = jnp.where((sources == slot)[..., None], tall[slot][None], padded)
    return padded


def unfold(padded, extent):
    windows = []
    for along_x in range(3):
        for along_y in range(3):
            for along_z in range(3):
                windows.append(
                    padded[
                        :,
                        along_x : along_x + extent,
                        along_y : along_y + extent,
                        along_z : along_z + extent,
                        :,
                    ]
                )
    stacked = jnp.concatenate(windows, axis=-1)
    return stacked.reshape(-1, stacked.shape[-1])


def into_cells(blocks, half_edge):
    slot_count, channels = (blocks.shape[0], blocks.shape[-1])
    lattice = blocks.reshape(slot_count, half_edge, 2, half_edge, 2, half_edge, 2, channels)
    lattice = lattice.transpose(0, 1, 3, 5, 2, 4, 6, 7)
    return lattice.reshape(slot_count * half_edge**3, 8 * channels)


def from_cells(cell_rows, slot_count, half_edge, channels):
    lattice = cell_rows.reshape(slot_count, half_edge, half_edge, half_edge, 2, 2, 2, channels)
    lattice = lattice.transpose(0, 1, 4, 2, 5, 3, 6, 7)
    return lattice.reshape(slot_count, 2 * half_edge, 2 * half_edge, 2 * half_edge, channels)


def silu_slope(values):
    logistic = jax.nn.sigmoid(values)
    return logistic * (1.0 + values * (1.0 - logistic))


def contract_rows(left, right):
    return lax.dot_general(
        left, right, (((0,), (0,)), ((), ())), preferred_element_type=jnp.float32
    )


def reduce_terms(terms):
    blocks = lax.axis_size("gx")
    quarters = lax.axis_size("gy")
    rows = [t.transpose(1, 0, 2).reshape(blocks, -1) for t in terms]
    packed = jnp.concatenate(rows, axis=1)
    width = packed.shape[1]
    packed = packed.reshape(blocks, quarters, width // quarters).transpose(1, 0, 2)
    part = lax.psum_scatter(packed.astype(jnp.bfloat16), "gy", scatter_dimension=0, tiled=True)
    part = part[0].astype(jnp.float32).reshape(blocks * 8, -1)
    part = lax.psum_scatter(part, "gx", scatter_dimension=0, tiled=True)
    row = lax.all_gather(part, "gy", axis=0, tiled=True).reshape(-1)
    out, start = [], 0
    for t in terms:
        size = t.size // blocks
        piece = row[start : start + size].reshape(t.shape[1] // blocks, t.shape[0], t.shape[2])
        out.append(piece.transpose(1, 0, 2))
        start += size
    return out


def body(features, cotangent, conv_first, down_weight, conv_second, block_count, neighbours):
    inputs = features[0, 0]
    slot_count, extent, channels = (inputs.shape[0], inputs.shape[1], inputs.shape[-1])
    half_edge = extent // 2
    wide_channels = conv_second.shape[-1]
    slot_table = neighbours[0, 0]
    live_mask = (jnp.arange(slot_count) < block_count[0, 0])[:, None, None, None, None]
    inputs = jnp.where(live_mask, inputs, jnp.zeros((), inputs.dtype))
    seed_blocks = jnp.where(live_mask, cotangent[0, 0], jnp.zeros((), inputs.dtype))
    sources_full = source_table(slot_table, extent)
    sources_half = source_table(slot_table, half_edge)

    wide_input, wide_seed = extend_xy([inputs, seed_blocks])
    first_cols = unfold(pad_field(wide_input, sources_full), extent)
    first_matrix = conv_first.reshape(-1, channels)
    pre_first = jnp.dot(first_cols, first_matrix, preferred_element_type=jnp.float32)
    hidden_first = jax.nn.silu(pre_first).astype(jnp.bfloat16)
    first_cells = into_cells(
        hidden_first.reshape(slot_count, extent, extent, extent, channels), half_edge
    )
    down_matrix = down_weight.reshape(-1, wide_channels)
    pre_down = jnp.dot(first_cells, down_matrix, preferred_element_type=jnp.float32)
    hidden_down = (
        jax.nn.silu(pre_down)
        .astype(jnp.bfloat16)
        .reshape(slot_count, half_edge, half_edge, half_edge, wide_channels)
    )
    (wide_hidden,) = extend_xy([hidden_down])
    second_cols = unfold(pad_field(wide_hidden, sources_half), half_edge)
    second_matrix = conv_second.reshape(-1, wide_channels)
    output_field = jnp.dot(second_cols, second_matrix, preferred_element_type=jnp.float32).astype(
        jnp.bfloat16
    )
    seed_cols = unfold(pad_field(wide_seed, sources_half), half_edge)
    second_flip = jnp.transpose(conv_second[::-1], (0, 2, 1)).reshape(-1, wide_channels)
    back_down = jnp.dot(seed_cols, second_flip, preferred_element_type=jnp.float32)
    delta_down = (back_down * silu_slope(pre_down)).astype(jnp.bfloat16)
    grad_second = contract_rows(second_cols, seed_blocks.reshape(-1, wide_channels))
    grad_down = contract_rows(first_cells, delta_down)
    second_sum, down_sum = reduce_terms(
        [
            grad_second.reshape(27, wide_channels, wide_channels),
            grad_down.reshape(8, channels, wide_channels),
        ]
    )
    back_cells = lax.dot_general(
        delta_down, down_matrix, (((1,), (1,)), ((), ())), preferred_element_type=jnp.float32
    )
    back_first = from_cells(back_cells, slot_count, half_edge, channels).reshape(-1, channels)
    delta_first = (back_first * silu_slope(pre_first)).astype(jnp.bfloat16)
    delta_blocks = delta_first.reshape(slot_count, extent, extent, extent, channels)
    (wide_delta,) = extend_xy([delta_blocks])
    delta_cols = unfold(pad_field(wide_delta, sources_full), extent)
    first_flip = jnp.transpose(conv_first[::-1], (0, 2, 1)).reshape(-1, channels)
    input_grad = jnp.dot(delta_cols, first_flip, preferred_element_type=jnp.float32).astype(
        jnp.bfloat16
    )
    grad_first = contract_rows(first_cols, delta_first)
    (first_sum,) = reduce_terms([grad_first.reshape(27, channels, channels)])
    devices = lax.axis_size("gx") * lax.axis_size("gy")
    scale_first = 1.0 / math.sqrt(float(devices * slot_count * extent**3))
    scale_half = 1.0 / math.sqrt(float(devices * slot_count * half_edge**3))
    return (
        output_field.reshape(1, 1, slot_count, half_edge, half_edge, half_edge, wide_channels),
        input_grad.reshape(1, 1, slot_count, extent, extent, extent, channels),
        first_sum * scale_first,
        down_sum * scale_half,
        second_sum * scale_half,
    )


def solution(mesh):
    placed = (
        P("gx", "gy", None, None, None, None, None),
        P("gx", "gy", None, None, None, None, None),
        P(),
        P(),
        P(),
        P("gx", "gy"),
        P("gx", "gy", None, None),
    )
    return jax.shard_map(
        body,
        mesh=mesh,
        in_specs=placed,
        out_specs=(
            P("gx", "gy", None, None, None, None, None),
            P("gx", "gy", None, None, None, None, None),
            P(None, "gx", None),
            P(None, "gx", None),
            P(None, "gx", None),
        ),
        check_vma=False,
    )
```

```python
import math

import jax
import jax.numpy as jnp
import numpy as np
from jax import lax
from jax.sharding import PartitionSpec as P


def shifted(block, axis, distance):
    devices = range(lax.axis_size(axis))
    route = [(i - distance, i) for i in devices if i - distance in devices]
    return lax.ppermute(block, axis, route)


def send_packed(pieces, axis, distance):
    flat = jnp.concatenate([piece.reshape(-1) for piece in pieces])
    arrived = shifted(flat, axis, distance)
    out, start = [], 0
    for piece in pieces:
        out.append(arrived[start : start + piece.size].reshape(piece.shape))
        start += piece.size
    return out


def extend_xy(fields):
    depth = [f.shape[1] for f in fields]
    from_left = send_packed([f[:, e - 1 : e] for f, e in zip(fields, depth)], "gx", 1)
    from_right = send_packed([f[:, 0:1] for f in fields], "gx", -1)
    wide = [jnp.concatenate([l, f, r], axis=1) for l, f, r in zip(from_left, fields, from_right)]
    from_down = send_packed([w[:, :, e - 1 : e] for w, e in zip(wide, depth)], "gy", 1)
    from_up = send_packed([w[:, :, 0:1] for w in wide], "gy", -1)
    return [jnp.concatenate([d, w, u], axis=2) for d, w, u in zip(from_down, wide, from_up)]


def source_table(slot_table, extent):
    slot_count = slot_table.shape[0]
    own = jnp.arange(slot_count, dtype=slot_table.dtype)[:, None]
    full = jnp.concatenate([slot_table[:, :13], own, slot_table[:, 13:]], axis=1)
    full = full.reshape(slot_count, 3, 3, 3)
    reps = np.array([1, extent, 1])
    for axis in (1, 2, 3):
        full = jnp.repeat(full, reps, axis=axis, total_repeat_length=extent + 2)
    return full


def pad_field(wide, sources):
    extent = wide.shape[3]
    tall = jnp.concatenate([wide[:, :, :, extent - 1 :], wide, wide[:, :, :, :1]], axis=3)
    padded = jnp.zeros((sources.shape[0],) + tall.shape[1:], tall.dtype)
    for slot in range(tall.shape[0]):
        padded = jnp.where((sources == slot)[..., None], tall[slot][None], padded)
    return padded


def unfold(padded, extent):
    windows = []
    for along_x in range(3):
        for along_y in range(3):
            for along_z in range(3):
                windows.append(
                    padded[
                        :,
                        along_x : along_x + extent,
                        along_y : along_y + extent,
                        along_z : along_z + extent,
                        :,
                    ]
                )
    stacked = jnp.concatenate(windows, axis=-1)
    return stacked.reshape(-1, stacked.shape[-1])


def into_cells(blocks, half_edge):
    slot_count, channels = (blocks.shape[0], blocks.shape[-1])
    lattice = blocks.reshape(slot_count, half_edge, 2, half_edge, 2, half_edge, 2, channels)
    lattice = lattice.transpose(0, 1, 3, 5, 2, 4, 6, 7)
    return lattice.reshape(slot_count * half_edge**3, 8 * channels)


def from_cells(cell_rows, slot_count, half_edge, channels):
    lattice = cell_rows.reshape(slot_count, half_edge, half_edge, half_edge, 2, 2, 2, channels)
    lattice = lattice.transpose(0, 1, 4, 2, 5, 3, 6, 7)
    return lattice.reshape(slot_count, 2 * half_edge, 2 * half_edge, 2 * half_edge, channels)


def silu_slope(values):
    logistic = jax.nn.sigmoid(values)
    return logistic * (1.0 + values * (1.0 - logistic))


def contract_rows(left, right):
    return lax.dot_general(
        left, right, (((0,), (0,)), ((), ())), preferred_element_type=jnp.float32
    )


def halving(data, axis, dtype):
    me = lax.axis_index(axis)
    size = lax.axis_size(axis)
    data = data.astype(dtype)
    distance = 1
    while distance < size and data.shape[0] > 1:
        bit = (me // distance) % 2
        pairs = data.reshape((data.shape[0] // 2, 2) + data.shape[1:])
        low, high = pairs[:, 0], pairs[:, 1]
        keep = jnp.where(bit == 0, low, high)
        send = jnp.where(bit == 0, high, low)
        route = [(i, i ^ distance) for i in range(size)]
        data = keep + lax.ppermute(send, axis, route)
        distance *= 2
    return data


def first_bit(data, axis, dtype):
    me = lax.axis_index(axis)
    size = lax.axis_size(axis)
    bit = me % 2
    pairs = data.astype(dtype).reshape((data.shape[0] // 2, 2) + data.shape[1:])
    low, high = pairs[:, 0], pairs[:, 1]
    keep = jnp.where(bit == 0, low, high)
    send = jnp.where(bit == 0, high, low)
    return keep + lax.ppermute(send, axis, [(i, i ^ 1) for i in range(size)])


def rest_bits(data, axis, dtype):
    me = lax.axis_index(axis)
    size = lax.axis_size(axis)
    data = data.astype(dtype)
    distance = 2
    while distance < size:
        bit = (me // distance) % 2
        pairs = data.reshape((data.shape[0] // 2, 2) + data.shape[1:])
        low, high = pairs[:, 0], pairs[:, 1]
        keep = jnp.where(bit == 0, low, high)
        send = jnp.where(bit == 0, high, low)
        data = keep + lax.ppermute(send, axis, [(i, i ^ distance) for i in range(size)])
        distance *= 2
    return data


def reduce_terms(terms):
    blocks = lax.axis_size("gx")
    quarters = lax.axis_size("gy")
    rows = [t.transpose(1, 0, 2).reshape(blocks, -1) for t in terms]
    packed = jnp.concatenate(rows, axis=1)
    width = packed.shape[1]
    packed = first_bit(packed, "gx", jnp.float32)
    packed = packed.reshape(blocks // 2, quarters, width // quarters).transpose(1, 0, 2)
    part = halving(packed, "gy", jnp.bfloat16)[0]
    part = rest_bits(part, "gx", jnp.float32)
    row = lax.all_gather(part, "gy", axis=0, tiled=True).reshape(-1)
    out, start = [], 0
    for t in terms:
        size = t.size // blocks
        piece = row[start : start + size].reshape(t.shape[1] // blocks, t.shape[0], t.shape[2])
        out.append(piece.transpose(1, 0, 2))
        start += size
    return out


def body(features, cotangent, conv_first, down_weight, conv_second, block_count, neighbours):
    inputs = features[0, 0]
    slot_count, extent, channels = (inputs.shape[0], inputs.shape[1], inputs.shape[-1])
    half_edge = extent // 2
    wide_channels = conv_second.shape[-1]
    slot_table = neighbours[0, 0]
    live_mask = (jnp.arange(slot_count) < block_count[0, 0])[:, None, None, None, None]
    inputs = jnp.where(live_mask, inputs, jnp.zeros((), inputs.dtype))
    seed_blocks = jnp.where(live_mask, cotangent[0, 0], jnp.zeros((), inputs.dtype))
    sources_full = source_table(slot_table, extent)
    sources_half = source_table(slot_table, half_edge)

    wide_input, wide_seed = extend_xy([inputs, seed_blocks])
    first_cols = unfold(pad_field(wide_input, sources_full), extent)
    first_matrix = conv_first.reshape(-1, channels)
    pre_first = jnp.dot(first_cols, first_matrix, preferred_element_type=jnp.float32)
    hidden_first = jax.nn.silu(pre_first).astype(jnp.bfloat16)
    first_cells = into_cells(
        hidden_first.reshape(slot_count, extent, extent, extent, channels), half_edge
    )
    down_matrix = down_weight.reshape(-1, wide_channels)
    pre_down = jnp.dot(first_cells, down_matrix, preferred_element_type=jnp.float32)
    hidden_down = (
        jax.nn.silu(pre_down)
        .astype(jnp.bfloat16)
        .reshape(slot_count, half_edge, half_edge, half_edge, wide_channels)
    )
    (wide_hidden,) = extend_xy([hidden_down])
    second_cols = unfold(pad_field(wide_hidden, sources_half), half_edge)
    second_matrix = conv_second.reshape(-1, wide_channels)
    output_field = jnp.dot(second_cols, second_matrix, preferred_element_type=jnp.float32).astype(
        jnp.bfloat16
    )
    seed_cols = unfold(pad_field(wide_seed, sources_half), half_edge)
    second_flip = jnp.transpose(conv_second[::-1], (0, 2, 1)).reshape(-1, wide_channels)
    back_down = jnp.dot(seed_cols, second_flip, preferred_element_type=jnp.float32)
    delta_down = (back_down * silu_slope(pre_down)).astype(jnp.bfloat16)
    grad_second = contract_rows(second_cols, seed_blocks.reshape(-1, wide_channels))
    grad_down = contract_rows(first_cells, delta_down)
    second_sum, down_sum = reduce_terms(
        [
            grad_second.reshape(27, wide_channels, wide_channels),
            grad_down.reshape(8, channels, wide_channels),
        ]
    )
    back_cells = lax.dot_general(
        delta_down, down_matrix, (((1,), (1,)), ((), ())), preferred_element_type=jnp.float32
    )
    back_first = from_cells(back_cells, slot_count, half_edge, channels).reshape(-1, channels)
    delta_first = (back_first * silu_slope(pre_first)).astype(jnp.bfloat16)
    delta_blocks = delta_first.reshape(slot_count, extent, extent, extent, channels)
    (wide_delta,) = extend_xy([delta_blocks])
    delta_cols = unfold(pad_field(wide_delta, sources_full), extent)
    first_flip = jnp.transpose(conv_first[::-1], (0, 2, 1)).reshape(-1, channels)
    input_grad = jnp.dot(delta_cols, first_flip, preferred_element_type=jnp.float32).astype(
        jnp.bfloat16
    )
    grad_first = contract_rows(first_cols, delta_first)
    (first_sum,) = reduce_terms([grad_first.reshape(27, channels, channels)])
    devices = lax.axis_size("gx") * lax.axis_size("gy")
    scale_first = 1.0 / math.sqrt(float(devices * slot_count * extent**3))
    scale_half = 1.0 / math.sqrt(float(devices * slot_count * half_edge**3))
    return (
        output_field.reshape(1, 1, slot_count, half_edge, half_edge, half_edge, wide_channels),
        input_grad.reshape(1, 1, slot_count, extent, extent, extent, channels),
        first_sum * scale_first,
        down_sum * scale_half,
        second_sum * scale_half,
    )


def solution(mesh):
    placed = (
        P("gx", "gy", None, None, None, None, None),
        P("gx", "gy", None, None, None, None, None),
        P(),
        P(),
        P(),
        P("gx", "gy"),
        P("gx", "gy", None, None),
    )
    return jax.shard_map(
        body,
        mesh=mesh,
        in_specs=placed,
        out_specs=(
            P("gx", "gy", None, None, None, None, None),
            P("gx", "gy", None, None, None, None, None),
            P(None, "gx", None),
            P(None, "gx", None),
            P(None, "gx", None),
        ),
        check_vma=False,
    )
```

```python
import math

import jax
import jax.numpy as jnp
import numpy as np
from jax import lax
from jax.sharding import PartitionSpec as P


def shifted(block, axis, distance):
    devices = range(lax.axis_size(axis))
    route = [(i - distance, i) for i in devices if i - distance in devices]
    return lax.ppermute(block, axis, route)


def send_packed(pieces, axis, distance):
    flat = jnp.concatenate([piece.reshape(-1) for piece in pieces])
    arrived = shifted(flat, axis, distance)
    out, start = [], 0
    for piece in pieces:
        out.append(arrived[start : start + piece.size].reshape(piece.shape))
        start += piece.size
    return out


def extend_xy(fields):
    depth = [f.shape[1] for f in fields]
    from_left = send_packed([f[:, e - 1 : e] for f, e in zip(fields, depth)], "gx", 1)
    from_right = send_packed([f[:, 0:1] for f in fields], "gx", -1)
    wide = [jnp.concatenate([l, f, r], axis=1) for l, f, r in zip(from_left, fields, from_right)]
    from_down = send_packed([w[:, :, e - 1 : e] for w, e in zip(wide, depth)], "gy", 1)
    from_up = send_packed([w[:, :, 0:1] for w in wide], "gy", -1)
    return [jnp.concatenate([d, w, u], axis=2) for d, w, u in zip(from_down, wide, from_up)]


def source_table(slot_table, extent):
    slot_count = slot_table.shape[0]
    own = jnp.arange(slot_count, dtype=slot_table.dtype)[:, None]
    full = jnp.concatenate([slot_table[:, :13], own, slot_table[:, 13:]], axis=1)
    full = full.reshape(slot_count, 3, 3, 3)
    reps = np.array([1, extent, 1])
    for axis in (1, 2, 3):
        full = jnp.repeat(full, reps, axis=axis, total_repeat_length=extent + 2)
    return full


def pad_field(wide, sources):
    extent = wide.shape[3]
    tall = jnp.concatenate([wide[:, :, :, extent - 1 :], wide, wide[:, :, :, :1]], axis=3)
    padded = jnp.zeros((sources.shape[0],) + tall.shape[1:], tall.dtype)
    for slot in range(tall.shape[0]):
        padded = jnp.where((sources == slot)[..., None], tall[slot][None], padded)
    return padded


def unfold(padded, extent):
    windows = []
    for along_x in range(3):
        for along_y in range(3):
            for along_z in range(3):
                windows.append(
                    padded[
                        :,
                        along_x : along_x + extent,
                        along_y : along_y + extent,
                        along_z : along_z + extent,
                        :,
                    ]
                )
    stacked = jnp.concatenate(windows, axis=-1)
    return stacked.reshape(-1, stacked.shape[-1])


def into_cells(blocks, half_edge):
    slot_count, channels = (blocks.shape[0], blocks.shape[-1])
    lattice = blocks.reshape(slot_count, half_edge, 2, half_edge, 2, half_edge, 2, channels)
    lattice = lattice.transpose(0, 1, 3, 5, 2, 4, 6, 7)
    return lattice.reshape(slot_count * half_edge**3, 8 * channels)


def from_cells(cell_rows, slot_count, half_edge, channels):
    lattice = cell_rows.reshape(slot_count, half_edge, half_edge, half_edge, 2, 2, 2, channels)
    lattice = lattice.transpose(0, 1, 4, 2, 5, 3, 6, 7)
    return lattice.reshape(slot_count, 2 * half_edge, 2 * half_edge, 2 * half_edge, channels)


def silu_slope(values):
    logistic = jax.nn.sigmoid(values)
    return logistic * (1.0 + values * (1.0 - logistic))


def contract_rows(left, right):
    return lax.dot_general(
        left, right, (((0,), (0,)), ((), ())), preferred_element_type=jnp.float32
    )


def halving(data, axis, dtype):
    me = lax.axis_index(axis)
    size = lax.axis_size(axis)
    data = data.astype(dtype)
    distance = 1
    while distance < size and data.shape[0] > 1:
        bit = (me // distance) % 2
        pairs = data.reshape((data.shape[0] // 2, 2) + data.shape[1:])
        keep = lax.dynamic_index_in_dim(pairs, bit, axis=1, keepdims=False)
        send = lax.dynamic_index_in_dim(pairs, 1 - bit, axis=1, keepdims=False)
        route = [(i, i ^ distance) for i in range(size)]
        data = keep + lax.ppermute(send, axis, route)
        distance *= 2
    return data


def first_bit(data, axis, dtype):
    me = lax.axis_index(axis)
    size = lax.axis_size(axis)
    bit = me % 2
    pairs = data.astype(dtype).reshape((data.shape[0] // 2, 2) + data.shape[1:])
    keep = lax.dynamic_index_in_dim(pairs, bit, axis=1, keepdims=False)
    send = lax.dynamic_index_in_dim(pairs, 1 - bit, axis=1, keepdims=False)
    return keep + lax.ppermute(send, axis, [(i, i ^ 1) for i in range(size)])


def rest_bits(data, axis, dtype):
    me = lax.axis_index(axis)
    size = lax.axis_size(axis)
    data = data.astype(dtype)
    distance = 2
    while distance < size:
        bit = (me // distance) % 2
        pairs = data.reshape((data.shape[0] // 2, 2) + data.shape[1:])
        keep = lax.dynamic_index_in_dim(pairs, bit, axis=1, keepdims=False)
        send = lax.dynamic_index_in_dim(pairs, 1 - bit, axis=1, keepdims=False)
        data = keep + lax.ppermute(send, axis, [(i, i ^ distance) for i in range(size)])
        distance *= 2
    return data


def reduce_terms(terms):
    blocks = lax.axis_size("gx")
    quarters = lax.axis_size("gy")
    rows = [t.transpose(1, 0, 2).reshape(blocks, -1) for t in terms]
    packed = jnp.concatenate(rows, axis=1)
    width = packed.shape[1]
    packed = first_bit(packed, "gx", jnp.float32)
    packed = packed.reshape(blocks // 2, quarters, width // quarters).transpose(1, 0, 2)
    part = halving(packed, "gy", jnp.bfloat16)[0]
    part = rest_bits(part, "gx", jnp.float32)
    row = lax.all_gather(part, "gy", axis=0, tiled=True).reshape(-1)
    out, start = [], 0
    for t in terms:
        size = t.size // blocks
        piece = row[start : start + size].reshape(t.shape[1] // blocks, t.shape[0], t.shape[2])
        out.append(piece.transpose(1, 0, 2))
        start += size
    return out


def body(features, cotangent, conv_first, down_weight, conv_second, block_count, neighbours):
    inputs = features[0, 0]
    slot_count, extent, channels = (inputs.shape[0], inputs.shape[1], inputs.shape[-1])
    half_edge = extent // 2
    wide_channels = conv_second.shape[-1]
    slot_table = neighbours[0, 0]
    live_mask = (jnp.arange(slot_count) < block_count[0, 0])[:, None, None, None, None]
    inputs = jnp.where(live_mask, inputs, jnp.zeros((), inputs.dtype))
    seed_blocks = jnp.where(live_mask, cotangent[0, 0], jnp.zeros((), inputs.dtype))
    sources_full = source_table(slot_table, extent)
    sources_half = source_table(slot_table, half_edge)

    wide_input, wide_seed = extend_xy([inputs, seed_blocks])
    first_cols = unfold(pad_field(wide_input, sources_full), extent)
    first_matrix = conv_first.reshape(-1, channels)
    pre_first = jnp.dot(first_cols, first_matrix, preferred_element_type=jnp.float32)
    hidden_first = jax.nn.silu(pre_first).astype(jnp.bfloat16)
    first_cells = into_cells(
        hidden_first.reshape(slot_count, extent, extent, extent, channels), half_edge
    )
    down_matrix = down_weight.reshape(-1, wide_channels)
    pre_down = jnp.dot(first_cells, down_matrix, preferred_element_type=jnp.float32)
    hidden_down = (
        jax.nn.silu(pre_down)
        .astype(jnp.bfloat16)
        .reshape(slot_count, half_edge, half_edge, half_edge, wide_channels)
    )
    (wide_hidden,) = extend_xy([hidden_down])
    second_cols = unfold(pad_field(wide_hidden, sources_half), half_edge)
    second_matrix = conv_second.reshape(-1, wide_channels)
    output_field = jnp.dot(second_cols, second_matrix, preferred_element_type=jnp.float32).astype(
        jnp.bfloat16
    )
    seed_cols = unfold(pad_field(wide_seed, sources_half), half_edge)
    second_flip = jnp.transpose(conv_second[::-1], (0, 2, 1)).reshape(-1, wide_channels)
    back_down = jnp.dot(seed_cols, second_flip, preferred_element_type=jnp.float32)
    delta_down = (back_down * silu_slope(pre_down)).astype(jnp.bfloat16)
    grad_second = contract_rows(second_cols, seed_blocks.reshape(-1, wide_channels))
    grad_down = contract_rows(first_cells, delta_down)
    back_cells = lax.dot_general(
        delta_down, down_matrix, (((1,), (1,)), ((), ())), preferred_element_type=jnp.float32
    )
    back_first = from_cells(back_cells, slot_count, half_edge, channels).reshape(-1, channels)
    delta_first = (back_first * silu_slope(pre_first)).astype(jnp.bfloat16)
    delta_blocks = delta_first.reshape(slot_count, extent, extent, extent, channels)
    (wide_delta,) = extend_xy([delta_blocks])
    delta_cols = unfold(pad_field(wide_delta, sources_full), extent)
    first_flip = jnp.transpose(conv_first[::-1], (0, 2, 1)).reshape(-1, channels)
    input_grad = jnp.dot(delta_cols, first_flip, preferred_element_type=jnp.float32).astype(
        jnp.bfloat16
    )
    grad_first = contract_rows(first_cols, delta_first)
    first_sum, second_sum, down_sum = reduce_terms(
        [
            grad_first.reshape(27, channels, channels),
            grad_second.reshape(27, wide_channels, wide_channels),
            grad_down.reshape(8, channels, wide_channels),
        ]
    )
    devices = lax.axis_size("gx") * lax.axis_size("gy")
    scale_first = 1.0 / math.sqrt(float(devices * slot_count * extent**3))
    scale_half = 1.0 / math.sqrt(float(devices * slot_count * half_edge**3))
    return (
        output_field.reshape(1, 1, slot_count, half_edge, half_edge, half_edge, wide_channels),
        input_grad.reshape(1, 1, slot_count, extent, extent, extent, channels),
        first_sum * scale_first,
        down_sum * scale_half,
        second_sum * scale_half,
    )


def solution(mesh):
    placed = (
        P("gx", "gy", None, None, None, None, None),
        P("gx", "gy", None, None, None, None, None),
        P(),
        P(),
        P(),
        P("gx", "gy"),
        P("gx", "gy", None, None),
    )
    return jax.shard_map(
        body,
        mesh=mesh,
        in_specs=placed,
        out_specs=(
            P("gx", "gy", None, None, None, None, None),
            P("gx", "gy", None, None, None, None, None),
            P(None, "gx", None),
            P(None, "gx", None),
            P(None, "gx", None),
        ),
        check_vma=False,
    )
```

```python
import math

import jax
import jax.numpy as jnp
import numpy as np
from jax import lax
from jax.sharding import PartitionSpec as P


def shifted(block, axis, distance):
    devices = range(lax.axis_size(axis))
    route = [(i - distance, i) for i in devices if i - distance in devices]
    return lax.ppermute(block, axis, route)


def send_packed(pieces, axis, distance):
    flat = jnp.concatenate([piece.reshape(-1) for piece in pieces])
    arrived = shifted(flat, axis, distance)
    out, start = [], 0
    for piece in pieces:
        out.append(arrived[start : start + piece.size].reshape(piece.shape))
        start += piece.size
    return out


def extend_xy(fields):
    depth = [f.shape[1] for f in fields]
    from_left = send_packed([f[:, e - 1 : e] for f, e in zip(fields, depth)], "gx", 1)
    from_right = send_packed([f[:, 0:1] for f in fields], "gx", -1)
    wide = [jnp.concatenate([l, f, r], axis=1) for l, f, r in zip(from_left, fields, from_right)]
    from_down = send_packed([w[:, :, e - 1 : e] for w, e in zip(wide, depth)], "gy", 1)
    from_up = send_packed([w[:, :, 0:1] for w in wide], "gy", -1)
    return [jnp.concatenate([d, w, u], axis=2) for d, w, u in zip(from_down, wide, from_up)]


def source_table(slot_table, extent):
    slot_count = slot_table.shape[0]
    own = jnp.arange(slot_count, dtype=slot_table.dtype)[:, None]
    full = jnp.concatenate([slot_table[:, :13], own, slot_table[:, 13:]], axis=1)
    full = full.reshape(slot_count, 3, 3, 3)
    reps = np.array([1, extent, 1])
    for axis in (1, 2, 3):
        full = jnp.repeat(full, reps, axis=axis, total_repeat_length=extent + 2)
    return full


def pad_field(wide, sources):
    extent = wide.shape[3]
    tall = jnp.concatenate([wide[:, :, :, extent - 1 :], wide, wide[:, :, :, :1]], axis=3)
    padded = jnp.zeros((sources.shape[0],) + tall.shape[1:], tall.dtype)
    for slot in range(tall.shape[0]):
        padded = jnp.where((sources == slot)[..., None], tall[slot][None], padded)
    return padded


def unfold(padded, extent):
    windows = []
    for along_x in range(3):
        for along_y in range(3):
            for along_z in range(3):
                windows.append(
                    padded[
                        :,
                        along_x : along_x + extent,
                        along_y : along_y + extent,
                        along_z : along_z + extent,
                        :,
                    ]
                )
    stacked = jnp.concatenate(windows, axis=-1)
    return stacked.reshape(-1, stacked.shape[-1])


def into_cells(blocks, half_edge):
    slot_count, channels = (blocks.shape[0], blocks.shape[-1])
    lattice = blocks.reshape(slot_count, half_edge, 2, half_edge, 2, half_edge, 2, channels)
    lattice = lattice.transpose(0, 1, 3, 5, 2, 4, 6, 7)
    return lattice.reshape(slot_count * half_edge**3, 8 * channels)


def from_cells(cell_rows, slot_count, half_edge, channels):
    lattice = cell_rows.reshape(slot_count, half_edge, half_edge, half_edge, 2, 2, 2, channels)
    lattice = lattice.transpose(0, 1, 4, 2, 5, 3, 6, 7)
    return lattice.reshape(slot_count, 2 * half_edge, 2 * half_edge, 2 * half_edge, channels)


def silu_slope(values):
    logistic = jax.nn.sigmoid(values)
    return logistic * (1.0 + values * (1.0 - logistic))


def contract_rows(left, right):
    return lax.dot_general(
        left, right, (((0,), (0,)), ((), ())), preferred_element_type=jnp.float32
    )


def halving(data, axis, dtype):
    me = lax.axis_index(axis)
    size = lax.axis_size(axis)
    data = data.astype(dtype)
    distance = 1
    while distance < size and data.shape[0] > 1:
        bit = (me // distance) % 2
        pairs = data.reshape((data.shape[0] // 2, 2) + data.shape[1:])
        keep = lax.dynamic_index_in_dim(pairs, bit, axis=1, keepdims=False)
        send = lax.dynamic_index_in_dim(pairs, 1 - bit, axis=1, keepdims=False)
        route = [(i, i ^ distance) for i in range(size)]
        data = keep + lax.ppermute(send, axis, route)
        distance *= 2
    return data


def first_bit(data, axis, dtype):
    me = lax.axis_index(axis)
    size = lax.axis_size(axis)
    bit = me % 2
    pairs = data.astype(dtype).reshape((data.shape[0] // 2, 2) + data.shape[1:])
    keep = lax.dynamic_index_in_dim(pairs, bit, axis=1, keepdims=False)
    send = lax.dynamic_index_in_dim(pairs, 1 - bit, axis=1, keepdims=False)
    return keep + lax.ppermute(send, axis, [(i, i ^ 1) for i in range(size)])


def rest_bits(data, axis, dtype, distances):
    me = lax.axis_index(axis)
    size = lax.axis_size(axis)
    data = data.astype(dtype)
    for distance in distances:
        bit = (me // distance) % 2
        pairs = data.reshape((data.shape[0] // 2, 2) + data.shape[1:])
        keep = lax.dynamic_index_in_dim(pairs, bit, axis=1, keepdims=False)
        send = lax.dynamic_index_in_dim(pairs, 1 - bit, axis=1, keepdims=False)
        data = keep + lax.ppermute(send, axis, [(i, i ^ distance) for i in range(size)])
    return data


def reduce_terms(terms):
    blocks = lax.axis_size("gx")
    quarters = lax.axis_size("gy")
    rows = [t.transpose(1, 0, 2).reshape(blocks, -1) for t in terms]
    packed = jnp.concatenate(rows, axis=1)
    width = packed.shape[1]
    packed = first_bit(packed, "gx", jnp.float32)
    bits = (blocks // 2).bit_length() - 1
    grid = packed.reshape((2,) * bits + (quarters, width // quarters))
    order = (bits, bits - 1) + tuple(range(bits - 1)) + (bits + 1,)
    packed = grid.transpose(order).reshape(quarters, blocks // 2, width // quarters)
    part = halving(packed, "gy", jnp.bfloat16)[0]
    distances = [2 ** k for k in range(2, bits + 1)] + [2]
    part = rest_bits(part, "gx", jnp.float32, distances)
    row = lax.all_gather(part, "gy", axis=0, tiled=True).reshape(-1)
    out, start = [], 0
    for t in terms:
        size = t.size // blocks
        piece = row[start : start + size].reshape(t.shape[1] // blocks, t.shape[0], t.shape[2])
        out.append(piece.transpose(1, 0, 2))
        start += size
    return out


def body(features, cotangent, conv_first, down_weight, conv_second, block_count, neighbours):
    inputs = features[0, 0]
    slot_count, extent, channels = (inputs.shape[0], inputs.shape[1], inputs.shape[-1])
    half_edge = extent // 2
    wide_channels = conv_second.shape[-1]
    slot_table = neighbours[0, 0]
    live_mask = (jnp.arange(slot_count) < block_count[0, 0])[:, None, None, None, None]
    inputs = jnp.where(live_mask, inputs, jnp.zeros((), inputs.dtype))
    seed_blocks = jnp.where(live_mask, cotangent[0, 0], jnp.zeros((), inputs.dtype))
    sources_full = source_table(slot_table, extent)
    sources_half = source_table(slot_table, half_edge)

    wide_input, wide_seed = extend_xy([inputs, seed_blocks])
    first_cols = unfold(pad_field(wide_input, sources_full), extent)
    first_matrix = conv_first.reshape(-1, channels)
    pre_first = jnp.dot(first_cols, first_matrix, preferred_element_type=jnp.float32)
    hidden_first = jax.nn.silu(pre_first).astype(jnp.bfloat16)
    first_cells = into_cells(
        hidden_first.reshape(slot_count, extent, extent, extent, channels), half_edge
    )
    down_matrix = down_weight.reshape(-1, wide_channels)
    pre_down = jnp.dot(first_cells, down_matrix, preferred_element_type=jnp.float32)
    hidden_down = (
        jax.nn.silu(pre_down)
        .astype(jnp.bfloat16)
        .reshape(slot_count, half_edge, half_edge, half_edge, wide_channels)
    )
    (wide_hidden,) = extend_xy([hidden_down])
    second_cols = unfold(pad_field(wide_hidden, sources_half), half_edge)
    second_matrix = conv_second.reshape(-1, wide_channels)
    output_field = jnp.dot(second_cols, second_matrix, preferred_element_type=jnp.float32).astype(
        jnp.bfloat16
    )
    seed_cols = unfold(pad_field(wide_seed, sources_half), half_edge)
    second_flip = jnp.transpose(conv_second[::-1], (0, 2, 1)).reshape(-1, wide_channels)
    back_down = jnp.dot(seed_cols, second_flip, preferred_element_type=jnp.float32)
    delta_down = (back_down * silu_slope(pre_down)).astype(jnp.bfloat16)
    grad_second = contract_rows(second_cols, seed_blocks.reshape(-1, wide_channels))
    grad_down = contract_rows(first_cells, delta_down)
    back_cells = lax.dot_general(
        delta_down, down_matrix, (((1,), (1,)), ((), ())), preferred_element_type=jnp.float32
    )
    back_first = from_cells(back_cells, slot_count, half_edge, channels).reshape(-1, channels)
    delta_first = (back_first * silu_slope(pre_first)).astype(jnp.bfloat16)
    delta_blocks = delta_first.reshape(slot_count, extent, extent, extent, channels)
    (wide_delta,) = extend_xy([delta_blocks])
    delta_cols = unfold(pad_field(wide_delta, sources_full), extent)
    first_flip = jnp.transpose(conv_first[::-1], (0, 2, 1)).reshape(-1, channels)
    input_grad = jnp.dot(delta_cols, first_flip, preferred_element_type=jnp.float32).astype(
        jnp.bfloat16
    )
    grad_first = contract_rows(first_cols, delta_first)
    first_sum, second_sum, down_sum = reduce_terms(
        [
            grad_first.reshape(27, channels, channels),
            grad_second.reshape(27, wide_channels, wide_channels),
            grad_down.reshape(8, channels, wide_channels),
        ]
    )
    devices = lax.axis_size("gx") * lax.axis_size("gy")
    scale_first = 1.0 / math.sqrt(float(devices * slot_count * extent**3))
    scale_half = 1.0 / math.sqrt(float(devices * slot_count * half_edge**3))
    return (
        output_field.reshape(1, 1, slot_count, half_edge, half_edge, half_edge, wide_channels),
        input_grad.reshape(1, 1, slot_count, extent, extent, extent, channels),
        first_sum * scale_first,
        down_sum * scale_half,
        second_sum * scale_half,
    )


def solution(mesh):
    placed = (
        P("gx", "gy", None, None, None, None, None),
        P("gx", "gy", None, None, None, None, None),
        P(),
        P(),
        P(),
        P("gx", "gy"),
        P("gx", "gy", None, None),
    )
    return jax.shard_map(
        body,
        mesh=mesh,
        in_specs=placed,
        out_specs=(
            P("gx", "gy", None, None, None, None, None),
            P("gx", "gy", None, None, None, None, None),
            P(None, "gx", None),
            P(None, "gx", None),
            P(None, "gx", None),
        ),
        check_vma=False,
    )
```

```python
import math

import jax
import jax.numpy as jnp
import numpy as np
from jax import lax
from jax.sharding import PartitionSpec as P


def shifted(block, axis, distance):
    devices = range(lax.axis_size(axis))
    route = [(i - distance, i) for i in devices if i - distance in devices]
    return lax.ppermute(block, axis, route)


def send_packed(pieces, axis, distance):
    flat = jnp.concatenate([piece.reshape(-1) for piece in pieces])
    arrived = shifted(flat, axis, distance)
    out, start = [], 0
    for piece in pieces:
        out.append(arrived[start : start + piece.size].reshape(piece.shape))
        start += piece.size
    return out


def extend_xy(fields):
    depth = [f.shape[1] for f in fields]
    from_left = send_packed([f[:, e - 1 : e] for f, e in zip(fields, depth)], "gx", 1)
    from_right = send_packed([f[:, 0:1] for f in fields], "gx", -1)
    wide = [jnp.concatenate([l, f, r], axis=1) for l, f, r in zip(from_left, fields, from_right)]
    from_down = send_packed([w[:, :, e - 1 : e] for w, e in zip(wide, depth)], "gy", 1)
    from_up = send_packed([w[:, :, 0:1] for w in wide], "gy", -1)
    return [jnp.concatenate([d, w, u], axis=2) for d, w, u in zip(from_down, wide, from_up)]


def source_table(slot_table, extent):
    slot_count = slot_table.shape[0]
    own = jnp.arange(slot_count, dtype=slot_table.dtype)[:, None]
    full = jnp.concatenate([slot_table[:, :13], own, slot_table[:, 13:]], axis=1)
    full = full.reshape(slot_count, 3, 3, 3)
    reps = np.array([1, extent, 1])
    for axis in (1, 2, 3):
        full = jnp.repeat(full, reps, axis=axis, total_repeat_length=extent + 2)
    return full


def pad_field(wide, sources):
    extent = wide.shape[3]
    tall = jnp.concatenate([wide[:, :, :, extent - 1 :], wide, wide[:, :, :, :1]], axis=3)
    padded = jnp.zeros((sources.shape[0],) + tall.shape[1:], tall.dtype)
    for slot in range(tall.shape[0]):
        padded = jnp.where((sources == slot)[..., None], tall[slot][None], padded)
    return padded


def unfold(padded, extent):
    windows = []
    for along_x in range(3):
        for along_y in range(3):
            for along_z in range(3):
                windows.append(
                    padded[
                        :,
                        along_x : along_x + extent,
                        along_y : along_y + extent,
                        along_z : along_z + extent,
                        :,
                    ]
                )
    stacked = jnp.concatenate(windows, axis=-1)
    return stacked.reshape(-1, stacked.shape[-1])


def into_cells(blocks, half_edge):
    slot_count, channels = (blocks.shape[0], blocks.shape[-1])
    lattice = blocks.reshape(slot_count, half_edge, 2, half_edge, 2, half_edge, 2, channels)
    lattice = lattice.transpose(0, 1, 3, 5, 2, 4, 6, 7)
    return lattice.reshape(slot_count * half_edge**3, 8 * channels)


def from_cells(cell_rows, slot_count, half_edge, channels):
    lattice = cell_rows.reshape(slot_count, half_edge, half_edge, half_edge, 2, 2, 2, channels)
    lattice = lattice.transpose(0, 1, 4, 2, 5, 3, 6, 7)
    return lattice.reshape(slot_count, 2 * half_edge, 2 * half_edge, 2 * half_edge, channels)


def conv3(padded, kernel):
    return lax.conv_general_dilated(
        padded,
        kernel,
        (1, 1, 1),
        "VALID",
        dimension_numbers=("NDHWC", "DHWIO", "NDHWC"),
        preferred_element_type=jnp.float32,
    )


def silu_slope(values):
    logistic = jax.nn.sigmoid(values)
    return logistic * (1.0 + values * (1.0 - logistic))


def contract_rows(left, right):
    return lax.dot_general(
        left, right, (((0,), (0,)), ((), ())), preferred_element_type=jnp.float32
    )


def halving(data, axis, dtype):
    me = lax.axis_index(axis)
    size = lax.axis_size(axis)
    data = data.astype(dtype)
    distance = 1
    while distance < size and data.shape[0] > 1:
        bit = (me // distance) % 2
        pairs = data.reshape((data.shape[0] // 2, 2) + data.shape[1:])
        keep = lax.dynamic_index_in_dim(pairs, bit, axis=1, keepdims=False)
        send = lax.dynamic_index_in_dim(pairs, 1 - bit, axis=1, keepdims=False)
        route = [(i, i ^ distance) for i in range(size)]
        data = keep + lax.ppermute(send, axis, route)
        distance *= 2
    return data


def first_bit(data, axis, dtype):
    me = lax.axis_index(axis)
    size = lax.axis_size(axis)
    bit = me % 2
    pairs = data.astype(dtype).reshape((data.shape[0] // 2, 2) + data.shape[1:])
    keep = lax.dynamic_index_in_dim(pairs, bit, axis=1, keepdims=False)
    send = lax.dynamic_index_in_dim(pairs, 1 - bit, axis=1, keepdims=False)
    return keep + lax.ppermute(send, axis, [(i, i ^ 1) for i in range(size)])


def rest_bits(data, axis, dtype, distances):
    me = lax.axis_index(axis)
    size = lax.axis_size(axis)
    data = data.astype(dtype)
    for distance in distances:
        bit = (me // distance) % 2
        pairs = data.reshape((data.shape[0] // 2, 2) + data.shape[1:])
        keep = lax.dynamic_index_in_dim(pairs, bit, axis=1, keepdims=False)
        send = lax.dynamic_index_in_dim(pairs, 1 - bit, axis=1, keepdims=False)
        data = keep + lax.ppermute(send, axis, [(i, i ^ distance) for i in range(size)])
    return data


def reduce_terms(terms):
    blocks = lax.axis_size("gx")
    quarters = lax.axis_size("gy")
    rows = [t.reshape(blocks, -1) for t in terms]
    packed = jnp.concatenate(rows, axis=1)
    width = packed.shape[1]
    packed = first_bit(packed, "gx", jnp.float32)
    bits = (blocks // 2).bit_length() - 1
    grid = packed.reshape((2,) * bits + (quarters, width // quarters))
    order = (bits, bits - 1) + tuple(range(bits - 1)) + (bits + 1,)
    packed = grid.transpose(order).reshape(quarters, blocks // 2, width // quarters)
    part = halving(packed, "gy", jnp.bfloat16)[0]
    distances = [2 ** k for k in range(2, bits + 1)] + [2]
    part = rest_bits(part, "gx", jnp.float32, distances)
    row = lax.all_gather(part, "gy", axis=0, tiled=True).reshape(-1)
    out, start = [], 0
    for t in terms:
        size = t.size // blocks
        piece = row[start : start + size].reshape(t.shape[0] // blocks, t.shape[1], t.shape[2])
        out.append(piece.transpose(1, 0, 2))
        start += size
    return out


def body(features, cotangent, conv_first, down_weight, conv_second, block_count, neighbours):
    inputs = features[0, 0]
    slot_count, extent, channels = (inputs.shape[0], inputs.shape[1], inputs.shape[-1])
    half_edge = extent // 2
    wide_channels = conv_second.shape[-1]
    slot_table = neighbours[0, 0]
    live_mask = (jnp.arange(slot_count) < block_count[0, 0])[:, None, None, None, None]
    inputs = jnp.where(live_mask, inputs, jnp.zeros((), inputs.dtype))
    seed_blocks = jnp.where(live_mask, cotangent[0, 0], jnp.zeros((), inputs.dtype))
    sources_full = source_table(slot_table, extent)
    sources_half = source_table(slot_table, half_edge)

    wide_input, wide_seed = extend_xy([inputs, seed_blocks])
    first_cols = unfold(pad_field(wide_input, sources_full), extent)
    first_matrix = conv_first.reshape(-1, channels)
    pre_first = jnp.dot(first_cols, first_matrix, preferred_element_type=jnp.float32)
    hidden_first = jax.nn.silu(pre_first).astype(jnp.bfloat16)
    first_cells = into_cells(
        hidden_first.reshape(slot_count, extent, extent, extent, channels), half_edge
    )
    down_matrix = down_weight.reshape(-1, wide_channels)
    pre_down = jnp.dot(first_cells, down_matrix, preferred_element_type=jnp.float32)
    hidden_down = (
        jax.nn.silu(pre_down)
        .astype(jnp.bfloat16)
        .reshape(slot_count, half_edge, half_edge, half_edge, wide_channels)
    )
    (wide_hidden,) = extend_xy([hidden_down])
    padded_hidden = pad_field(wide_hidden, sources_half)
    kernel_shape = (3, 3, 3, wide_channels, wide_channels)
    output_field = conv3(padded_hidden, conv_second.reshape(kernel_shape)).astype(jnp.bfloat16)
    second_flip = jnp.transpose(conv_second[::-1], (0, 2, 1)).reshape(kernel_shape)
    back_down = conv3(pad_field(wide_seed, sources_half), second_flip).reshape(-1, wide_channels)
    delta_down = (back_down * silu_slope(pre_down)).astype(jnp.bfloat16)
    grad_second = lax.conv_general_dilated(
        padded_hidden,
        seed_blocks,
        (1, 1, 1),
        "VALID",
        dimension_numbers=("CDHWN", "IDHWO", "NDHWC"),
        preferred_element_type=jnp.float32,
    )
    grad_down = contract_rows(first_cells, delta_down)
    back_cells = lax.dot_general(
        delta_down, down_matrix, (((1,), (1,)), ((), ())), preferred_element_type=jnp.float32
    )
    back_first = from_cells(back_cells, slot_count, half_edge, channels).reshape(-1, channels)
    delta_first = (back_first * silu_slope(pre_first)).astype(jnp.bfloat16)
    delta_blocks = delta_first.reshape(slot_count, extent, extent, extent, channels)
    (wide_delta,) = extend_xy([delta_blocks])
    delta_cols = unfold(pad_field(wide_delta, sources_full), extent)
    first_flip = jnp.transpose(conv_first[::-1], (0, 2, 1)).reshape(-1, channels)
    input_grad = jnp.dot(delta_cols, first_flip, preferred_element_type=jnp.float32).astype(
        jnp.bfloat16
    )
    grad_first = contract_rows(first_cols, delta_first)
    first_sum, second_sum, down_sum = reduce_terms(
        [
            grad_first.reshape(27, channels, channels).transpose(1, 0, 2),
            grad_second.reshape(wide_channels, 27, wide_channels),
            grad_down.reshape(8, channels, wide_channels).transpose(1, 0, 2),
        ]
    )
    devices = lax.axis_size("gx") * lax.axis_size("gy")
    scale_first = 1.0 / math.sqrt(float(devices * slot_count * extent**3))
    scale_half = 1.0 / math.sqrt(float(devices * slot_count * half_edge**3))
    return (
        output_field.reshape(1, 1, slot_count, half_edge, half_edge, half_edge, wide_channels),
        input_grad.reshape(1, 1, slot_count, extent, extent, extent, channels),
        first_sum * scale_first,
        down_sum * scale_half,
        second_sum * scale_half,
    )


def solution(mesh):
    placed = (
        P("gx", "gy", None, None, None, None, None),
        P("gx", "gy", None, None, None, None, None),
        P(),
        P(),
        P(),
        P("gx", "gy"),
        P("gx", "gy", None, None),
    )
    return jax.shard_map(
        body,
        mesh=mesh,
        in_specs=placed,
        out_specs=(
            P("gx", "gy", None, None, None, None, None),
            P("gx", "gy", None, None, None, None, None),
            P(None, "gx", None),
            P(None, "gx", None),
            P(None, "gx", None),
        ),
        check_vma=False,
    )
```

```python
import math

import jax
import jax.numpy as jnp
import numpy as np
from jax import lax
from jax.sharding import PartitionSpec as P


def shifted(block, axis, distance):
    devices = range(lax.axis_size(axis))
    route = [(i - distance, i) for i in devices if i - distance in devices]
    return lax.ppermute(block, axis, route)


def send_packed(pieces, axis, distance):
    flat = jnp.concatenate([piece.reshape(-1) for piece in pieces])
    arrived = shifted(flat, axis, distance)
    out, start = [], 0
    for piece in pieces:
        out.append(arrived[start : start + piece.size].reshape(piece.shape))
        start += piece.size
    return out


def extend_xy(fields):
    depth = [f.shape[1] for f in fields]
    from_left = send_packed([f[:, e - 1 : e] for f, e in zip(fields, depth)], "gx", 1)
    from_right = send_packed([f[:, 0:1] for f in fields], "gx", -1)
    wide = [jnp.concatenate([l, f, r], axis=1) for l, f, r in zip(from_left, fields, from_right)]
    from_down = send_packed([w[:, :, e - 1 : e] for w, e in zip(wide, depth)], "gy", 1)
    from_up = send_packed([w[:, :, 0:1] for w in wide], "gy", -1)
    return [jnp.concatenate([d, w, u], axis=2) for d, w, u in zip(from_down, wide, from_up)]


def source_table(slot_table, extent):
    slot_count = slot_table.shape[0]
    own = jnp.arange(slot_count, dtype=slot_table.dtype)[:, None]
    full = jnp.concatenate([slot_table[:, :13], own, slot_table[:, 13:]], axis=1)
    full = full.reshape(slot_count, 3, 3, 3)
    reps = np.array([1, extent, 1])
    for axis in (1, 2, 3):
        full = jnp.repeat(full, reps, axis=axis, total_repeat_length=extent + 2)
    return full


def pad_field(wide, sources):
    extent = wide.shape[3]
    tall = jnp.concatenate([wide[:, :, :, extent - 1 :], wide, wide[:, :, :, :1]], axis=3)
    padded = jnp.zeros((sources.shape[0],) + tall.shape[1:], tall.dtype)
    for slot in range(tall.shape[0]):
        padded = jnp.where((sources == slot)[..., None], tall[slot][None], padded)
    return padded


def unfold(padded, extent):
    windows = []
    for along_x in range(3):
        for along_y in range(3):
            for along_z in range(3):
                windows.append(
                    padded[
                        :,
                        along_x : along_x + extent,
                        along_y : along_y + extent,
                        along_z : along_z + extent,
                        :,
                    ]
                )
    stacked = jnp.concatenate(windows, axis=-1)
    return stacked.reshape(-1, stacked.shape[-1])


def into_cells(blocks, half_edge):
    slot_count, channels = (blocks.shape[0], blocks.shape[-1])
    lattice = blocks.reshape(slot_count, half_edge, 2, half_edge, 2, half_edge, 2, channels)
    lattice = lattice.transpose(0, 1, 3, 5, 2, 4, 6, 7)
    return lattice.reshape(slot_count * half_edge**3, 8 * channels)


def from_cells(cell_rows, slot_count, half_edge, channels):
    lattice = cell_rows.reshape(slot_count, half_edge, half_edge, half_edge, 2, 2, 2, channels)
    lattice = lattice.transpose(0, 1, 4, 2, 5, 3, 6, 7)
    return lattice.reshape(slot_count, 2 * half_edge, 2 * half_edge, 2 * half_edge, channels)


def conv3(padded, kernel):
    return lax.conv_general_dilated(
        padded,
        kernel,
        (1, 1, 1),
        "VALID",
        dimension_numbers=("NDHWC", "DHWIO", "NDHWC"),
        preferred_element_type=jnp.float32,
    )


def silu_slope(values):
    logistic = jax.nn.sigmoid(values)
    return logistic * (1.0 + values * (1.0 - logistic))


def contract_rows(left, right):
    return lax.dot_general(
        left, right, (((0,), (0,)), ((), ())), preferred_element_type=jnp.float32
    )


def halving(data, axis, dtype):
    me = lax.axis_index(axis)
    size = lax.axis_size(axis)
    data = data.astype(dtype)
    distance = 1
    while distance < size and data.shape[0] > 1:
        bit = (me // distance) % 2
        pairs = data.reshape((data.shape[0] // 2, 2) + data.shape[1:])
        keep = lax.dynamic_index_in_dim(pairs, bit, axis=1, keepdims=False)
        send = lax.dynamic_index_in_dim(pairs, 1 - bit, axis=1, keepdims=False)
        route = [(i, i ^ distance) for i in range(size)]
        data = keep + lax.ppermute(send, axis, route)
        distance *= 2
    return data


def first_bit(data, axis, dtype):
    me = lax.axis_index(axis)
    size = lax.axis_size(axis)
    bit = me % 2
    pairs = data.astype(dtype).reshape((data.shape[0] // 2, 2) + data.shape[1:])
    keep = lax.dynamic_index_in_dim(pairs, bit, axis=1, keepdims=False)
    send = lax.dynamic_index_in_dim(pairs, 1 - bit, axis=1, keepdims=False)
    return keep + lax.ppermute(send, axis, [(i, i ^ 1) for i in range(size)])


def rest_bits(data, axis, dtype, distances):
    me = lax.axis_index(axis)
    size = lax.axis_size(axis)
    data = data.astype(dtype)
    for distance in distances:
        bit = (me // distance) % 2
        pairs = data.reshape((data.shape[0] // 2, 2) + data.shape[1:])
        keep = lax.dynamic_index_in_dim(pairs, bit, axis=1, keepdims=False)
        send = lax.dynamic_index_in_dim(pairs, 1 - bit, axis=1, keepdims=False)
        data = keep + lax.ppermute(send, axis, [(i, i ^ distance) for i in range(size)])
    return data


def reduce_terms(terms):
    blocks = lax.axis_size("gx")
    quarters = lax.axis_size("gy")
    rows = [t.reshape(blocks, -1) for t in terms]
    packed = jnp.concatenate(rows, axis=1)
    width = packed.shape[1]
    packed = first_bit(packed, "gx", jnp.float32)
    bits = (blocks // 2).bit_length() - 1
    grid = packed.reshape((2,) * bits + (quarters, width // quarters))
    order = (bits, bits - 1) + tuple(range(bits - 1)) + (bits + 1,)
    packed = grid.transpose(order).reshape(quarters, blocks // 2, width // quarters)
    part = halving(packed, "gy", jnp.bfloat16)[0]
    distances = [2 ** k for k in range(2, bits + 1)] + [2]
    part = rest_bits(part, "gx", jnp.float32, distances)
    row = lax.all_gather(part, "gy", axis=0, tiled=True).reshape(-1)
    out, start = [], 0
    for t in terms:
        size = t.size // blocks
        piece = row[start : start + size].reshape(t.shape[0] // blocks, t.shape[1], t.shape[2])
        out.append(piece.transpose(1, 0, 2))
        start += size
    return out


def body(features, cotangent, conv_first, down_weight, conv_second, block_count, neighbours):
    inputs = features[0, 0]
    slot_count, extent, channels = (inputs.shape[0], inputs.shape[1], inputs.shape[-1])
    half_edge = extent // 2
    wide_channels = conv_second.shape[-1]
    slot_table = neighbours[0, 0]
    live_mask = (jnp.arange(slot_count) < block_count[0, 0])[:, None, None, None, None]
    inputs = jnp.where(live_mask, inputs, jnp.zeros((), inputs.dtype))
    seed_blocks = jnp.where(live_mask, cotangent[0, 0], jnp.zeros((), inputs.dtype))
    sources_full = source_table(slot_table, extent)
    sources_half = source_table(slot_table, half_edge)

    wide_input, wide_seed = extend_xy([inputs, seed_blocks])
    padded_input = pad_field(wide_input, sources_full)
    first_shape = (3, 3, 3, channels, channels)
    pre_first = conv3(padded_input, conv_first.reshape(first_shape)).reshape(-1, channels)
    hidden_first = jax.nn.silu(pre_first).astype(jnp.bfloat16)
    first_cells = into_cells(
        hidden_first.reshape(slot_count, extent, extent, extent, channels), half_edge
    )
    down_matrix = down_weight.reshape(-1, wide_channels)
    pre_down = jnp.dot(first_cells, down_matrix, preferred_element_type=jnp.float32)
    hidden_down = (
        jax.nn.silu(pre_down)
        .astype(jnp.bfloat16)
        .reshape(slot_count, half_edge, half_edge, half_edge, wide_channels)
    )
    (wide_hidden,) = extend_xy([hidden_down])
    padded_hidden = pad_field(wide_hidden, sources_half)
    kernel_shape = (3, 3, 3, wide_channels, wide_channels)
    output_field = conv3(padded_hidden, conv_second.reshape(kernel_shape)).astype(jnp.bfloat16)
    second_flip = jnp.transpose(conv_second[::-1], (0, 2, 1)).reshape(kernel_shape)
    back_down = conv3(pad_field(wide_seed, sources_half), second_flip).reshape(-1, wide_channels)
    delta_down = (back_down * silu_slope(pre_down)).astype(jnp.bfloat16)
    grad_second = lax.conv_general_dilated(
        padded_hidden,
        seed_blocks,
        (1, 1, 1),
        "VALID",
        dimension_numbers=("CDHWN", "IDHWO", "NDHWC"),
        preferred_element_type=jnp.float32,
    )
    grad_down = contract_rows(first_cells, delta_down)
    back_cells = lax.dot_general(
        delta_down, down_matrix, (((1,), (1,)), ((), ())), preferred_element_type=jnp.float32
    )
    back_first = from_cells(back_cells, slot_count, half_edge, channels).reshape(-1, channels)
    delta_first = (back_first * silu_slope(pre_first)).astype(jnp.bfloat16)
    delta_blocks = delta_first.reshape(slot_count, extent, extent, extent, channels)
    (wide_delta,) = extend_xy([delta_blocks])
    first_flip = jnp.transpose(conv_first[::-1], (0, 2, 1)).reshape(first_shape)
    input_grad = conv3(pad_field(wide_delta, sources_full), first_flip).astype(jnp.bfloat16)
    grad_first = lax.conv_general_dilated(
        padded_input,
        delta_blocks,
        (1, 1, 1),
        "VALID",
        dimension_numbers=("CDHWN", "IDHWO", "NDHWC"),
        preferred_element_type=jnp.float32,
    )
    first_sum, second_sum, down_sum = reduce_terms(
        [
            grad_first.reshape(channels, 27, channels),
            grad_second.reshape(wide_channels, 27, wide_channels),
            grad_down.reshape(8, channels, wide_channels).transpose(1, 0, 2),
        ]
    )
    devices = lax.axis_size("gx") * lax.axis_size("gy")
    scale_first = 1.0 / math.sqrt(float(devices * slot_count * extent**3))
    scale_half = 1.0 / math.sqrt(float(devices * slot_count * half_edge**3))
    return (
        output_field.reshape(1, 1, slot_count, half_edge, half_edge, half_edge, wide_channels),
        input_grad.reshape(1, 1, slot_count, extent, extent, extent, channels),
        first_sum * scale_first,
        down_sum * scale_half,
        second_sum * scale_half,
    )


def solution(mesh):
    placed = (
        P("gx", "gy", None, None, None, None, None),
        P("gx", "gy", None, None, None, None, None),
        P(),
        P(),
        P(),
        P("gx", "gy"),
        P("gx", "gy", None, None),
    )
    return jax.shard_map(
        body,
        mesh=mesh,
        in_specs=placed,
        out_specs=(
            P("gx", "gy", None, None, None, None, None),
            P("gx", "gy", None, None, None, None, None),
            P(None, "gx", None),
            P(None, "gx", None),
            P(None, "gx", None),
        ),
        check_vma=False,
    )
```

```python
import math

import jax
import jax.numpy as jnp
import numpy as np
from jax import lax
from jax.sharding import PartitionSpec as P


def shifted(block, axis, distance):
    devices = range(lax.axis_size(axis))
    route = [(i - distance, i) for i in devices if i - distance in devices]
    return lax.ppermute(block, axis, route)


def send_packed(pieces, axis, distance):
    flat = jnp.concatenate([piece.reshape(-1) for piece in pieces])
    arrived = shifted(flat, axis, distance)
    out, start = [], 0
    for piece in pieces:
        out.append(arrived[start : start + piece.size].reshape(piece.shape))
        start += piece.size
    return out


def extend_xy(fields):
    depth = [f.shape[1] for f in fields]
    from_left = send_packed([f[:, e - 1 : e] for f, e in zip(fields, depth)], "gx", 1)
    from_right = send_packed([f[:, 0:1] for f in fields], "gx", -1)
    wide = [jnp.concatenate([l, f, r], axis=1) for l, f, r in zip(from_left, fields, from_right)]
    from_down = send_packed([w[:, :, e - 1 : e] for w, e in zip(wide, depth)], "gy", 1)
    from_up = send_packed([w[:, :, 0:1] for w in wide], "gy", -1)
    return [jnp.concatenate([d, w, u], axis=2) for d, w, u in zip(from_down, wide, from_up)]


def source_table(slot_table, extent):
    slot_count = slot_table.shape[0]
    own = jnp.arange(slot_count, dtype=slot_table.dtype)[:, None]
    full = jnp.concatenate([slot_table[:, :13], own, slot_table[:, 13:]], axis=1)
    full = full.reshape(slot_count, 3, 3, 3)
    reps = np.array([1, extent, 1])
    for axis in (1, 2, 3):
        full = jnp.repeat(full, reps, axis=axis, total_repeat_length=extent + 2)
    return full


def pad_field(wide, sources):
    extent = wide.shape[3]
    tall = jnp.concatenate([wide[:, :, :, extent - 1 :], wide, wide[:, :, :, :1]], axis=3)
    padded = jnp.zeros((sources.shape[0],) + tall.shape[1:], tall.dtype)
    for slot in range(tall.shape[0]):
        padded = jnp.where((sources == slot)[..., None], tall[slot][None], padded)
    return padded


def into_cells(blocks, half_edge):
    slot_count, channels = (blocks.shape[0], blocks.shape[-1])
    lattice = blocks.reshape(slot_count, half_edge, 2, half_edge, 2, half_edge, 2, channels)
    lattice = lattice.transpose(0, 1, 3, 5, 2, 4, 6, 7)
    return lattice.reshape(slot_count * half_edge**3, 8 * channels)


def from_cells(cell_rows, slot_count, half_edge, channels):
    lattice = cell_rows.reshape(slot_count, half_edge, half_edge, half_edge, 2, 2, 2, channels)
    lattice = lattice.transpose(0, 1, 4, 2, 5, 3, 6, 7)
    return lattice.reshape(slot_count, 2 * half_edge, 2 * half_edge, 2 * half_edge, channels)


def conv3(padded, kernel):
    return lax.conv_general_dilated(
        padded,
        kernel,
        (1, 1, 1),
        "VALID",
        dimension_numbers=("NDHWC", "DHWIO", "NDHWC"),
        preferred_element_type=jnp.float32,
    )


def silu_slope(values):
    logistic = jax.nn.sigmoid(values)
    return logistic * (1.0 + values * (1.0 - logistic))


def contract_rows(left, right):
    return lax.dot_general(
        left, right, (((0,), (0,)), ((), ())), preferred_element_type=jnp.float32
    )


def halving(data, axis, dtype):
    me = lax.axis_index(axis)
    size = lax.axis_size(axis)
    data = data.astype(dtype)
    distance = 1
    while distance < size and data.shape[0] > 1:
        bit = (me // distance) % 2
        pairs = data.reshape((data.shape[0] // 2, 2) + data.shape[1:])
        keep = lax.dynamic_index_in_dim(pairs, bit, axis=1, keepdims=False)
        send = lax.dynamic_index_in_dim(pairs, 1 - bit, axis=1, keepdims=False)
        route = [(i, i ^ distance) for i in range(size)]
        data = keep + lax.ppermute(send, axis, route)
        distance *= 2
    return data


def first_bit(data, axis, dtype):
    me = lax.axis_index(axis)
    size = lax.axis_size(axis)
    bit = me % 2
    pairs = data.astype(dtype).reshape((data.shape[0] // 2, 2) + data.shape[1:])
    keep = lax.dynamic_index_in_dim(pairs, bit, axis=1, keepdims=False)
    send = lax.dynamic_index_in_dim(pairs, 1 - bit, axis=1, keepdims=False)
    return keep + lax.ppermute(send, axis, [(i, i ^ 1) for i in range(size)])


def rest_bits(data, axis, dtype, distances):
    me = lax.axis_index(axis)
    size = lax.axis_size(axis)
    data = data.astype(dtype)
    for distance in distances:
        bit = (me // distance) % 2
        pairs = data.reshape((data.shape[0] // 2, 2) + data.shape[1:])
        keep = lax.dynamic_index_in_dim(pairs, bit, axis=1, keepdims=False)
        send = lax.dynamic_index_in_dim(pairs, 1 - bit, axis=1, keepdims=False)
        data = keep + lax.ppermute(send, axis, [(i, i ^ distance) for i in range(size)])
    return data


def reduce_terms(terms):
    blocks = lax.axis_size("gx")
    quarters = lax.axis_size("gy")
    rows = [t.reshape(blocks, -1) for t in terms]
    packed = jnp.concatenate(rows, axis=1)
    width = packed.shape[1]
    packed = first_bit(packed, "gx", jnp.bfloat16)
    bits = (blocks // 2).bit_length() - 1
    grid = packed.reshape((2,) * bits + (quarters, width // quarters))
    order = (bits, bits - 1) + tuple(range(bits - 1)) + (bits + 1,)
    packed = grid.transpose(order).reshape(quarters, blocks // 2, width // quarters)
    part = halving(packed, "gy", jnp.bfloat16)[0]
    distances = [2 ** k for k in range(2, bits + 1)] + [2]
    part = rest_bits(part, "gx", jnp.float32, distances)
    row = lax.all_gather(part, "gy", axis=0, tiled=True).reshape(-1)
    out, start = [], 0
    for t in terms:
        size = t.size // blocks
        piece = row[start : start + size].reshape(t.shape[0] // blocks, t.shape[1], t.shape[2])
        out.append(piece.transpose(1, 0, 2))
        start += size
    return out


def body(features, cotangent, conv_first, down_weight, conv_second, block_count, neighbours):
    inputs = features[0, 0]
    slot_count, extent, channels = (inputs.shape[0], inputs.shape[1], inputs.shape[-1])
    half_edge = extent // 2
    wide_channels = conv_second.shape[-1]
    slot_table = neighbours[0, 0]
    live_mask = (jnp.arange(slot_count) < block_count[0, 0])[:, None, None, None, None]
    inputs = jnp.where(live_mask, inputs, jnp.zeros((), inputs.dtype))
    seed_blocks = jnp.where(live_mask, cotangent[0, 0], jnp.zeros((), inputs.dtype))
    sources_full = source_table(slot_table, extent)
    sources_half = source_table(slot_table, half_edge)

    wide_input, wide_seed = extend_xy([inputs, seed_blocks])
    padded_input = pad_field(wide_input, sources_full)
    first_shape = (3, 3, 3, channels, channels)
    pre_first = conv3(padded_input, conv_first.reshape(first_shape)).reshape(-1, channels)
    hidden_first = jax.nn.silu(pre_first).astype(jnp.bfloat16)
    first_cells = into_cells(
        hidden_first.reshape(slot_count, extent, extent, extent, channels), half_edge
    )
    down_matrix = down_weight.reshape(-1, wide_channels)
    pre_down = jnp.dot(first_cells, down_matrix, preferred_element_type=jnp.float32)
    hidden_down = (
        jax.nn.silu(pre_down)
        .astype(jnp.bfloat16)
        .reshape(slot_count, half_edge, half_edge, half_edge, wide_channels)
    )
    (wide_hidden,) = extend_xy([hidden_down])
    padded_hidden = pad_field(wide_hidden, sources_half)
    kernel_shape = (3, 3, 3, wide_channels, wide_channels)
    output_field = conv3(padded_hidden, conv_second.reshape(kernel_shape)).astype(jnp.bfloat16)
    second_flip = jnp.transpose(conv_second[::-1], (0, 2, 1)).reshape(kernel_shape)
    back_down = conv3(pad_field(wide_seed, sources_half), second_flip).reshape(-1, wide_channels)
    delta_down = (back_down * silu_slope(pre_down)).astype(jnp.bfloat16)
    grad_second = lax.conv_general_dilated(
        padded_hidden,
        seed_blocks,
        (1, 1, 1),
        "VALID",
        dimension_numbers=("CDHWN", "IDHWO", "NDHWC"),
        preferred_element_type=jnp.float32,
    )
    grad_down = contract_rows(first_cells, delta_down)
    back_cells = lax.dot_general(
        delta_down, down_matrix, (((1,), (1,)), ((), ())), preferred_element_type=jnp.float32
    )
    back_first = from_cells(back_cells, slot_count, half_edge, channels).reshape(-1, channels)
    delta_first = (back_first * silu_slope(pre_first)).astype(jnp.bfloat16)
    delta_blocks = delta_first.reshape(slot_count, extent, extent, extent, channels)
    (wide_delta,) = extend_xy([delta_blocks])
    first_flip = jnp.transpose(conv_first[::-1], (0, 2, 1)).reshape(first_shape)
    input_grad = conv3(pad_field(wide_delta, sources_full), first_flip).astype(jnp.bfloat16)
    grad_first = lax.conv_general_dilated(
        padded_input,
        delta_blocks,
        (1, 1, 1),
        "VALID",
        dimension_numbers=("CDHWN", "IDHWO", "NDHWC"),
        preferred_element_type=jnp.float32,
    )
    first_sum, second_sum, down_sum = reduce_terms(
        [
            grad_first.reshape(channels, 27, channels),
            grad_second.reshape(wide_channels, 27, wide_channels),
            grad_down.reshape(8, channels, wide_channels).transpose(1, 0, 2),
        ]
    )
    devices = lax.axis_size("gx") * lax.axis_size("gy")
    scale_first = 1.0 / math.sqrt(float(devices * slot_count * extent**3))
    scale_half = 1.0 / math.sqrt(float(devices * slot_count * half_edge**3))
    return (
        output_field.reshape(1, 1, slot_count, half_edge, half_edge, half_edge, wide_channels),
        input_grad.reshape(1, 1, slot_count, extent, extent, extent, channels),
        first_sum * scale_first,
        down_sum * scale_half,
        second_sum * scale_half,
    )


def solution(mesh):
    placed = (
        P("gx", "gy", None, None, None, None, None),
        P("gx", "gy", None, None, None, None, None),
        P(),
        P(),
        P(),
        P("gx", "gy"),
        P("gx", "gy", None, None),
    )
    return jax.shard_map(
        body,
        mesh=mesh,
        in_specs=placed,
        out_specs=(
            P("gx", "gy", None, None, None, None, None),
            P("gx", "gy", None, None, None, None, None),
            P(None, "gx", None),
            P(None, "gx", None),
            P(None, "gx", None),
        ),
        check_vma=False,
    )
```

```python
import math

import jax
import jax.numpy as jnp
import numpy as np
from jax import lax
from jax.sharding import PartitionSpec as P


def shifted(block, axis, distance):
    devices = range(lax.axis_size(axis))
    route = [(i - distance, i) for i in devices if i - distance in devices]
    return lax.ppermute(block, axis, route)


def send_packed(pieces, axis, distance):
    flat = jnp.concatenate([piece.reshape(-1) for piece in pieces])
    arrived = shifted(flat, axis, distance)
    out, start = [], 0
    for piece in pieces:
        out.append(arrived[start : start + piece.size].reshape(piece.shape))
        start += piece.size
    return out


def extend_xy(fields):
    depth = [f.shape[1] for f in fields]
    from_left = send_packed([f[:, e - 1 : e] for f, e in zip(fields, depth)], "gx", 1)
    from_right = send_packed([f[:, 0:1] for f in fields], "gx", -1)
    wide = [jnp.concatenate([l, f, r], axis=1) for l, f, r in zip(from_left, fields, from_right)]
    from_down = send_packed([w[:, :, e - 1 : e] for w, e in zip(wide, depth)], "gy", 1)
    from_up = send_packed([w[:, :, 0:1] for w in wide], "gy", -1)
    return [jnp.concatenate([d, w, u], axis=2) for d, w, u in zip(from_down, wide, from_up)]


def source_table(slot_table, extent):
    slot_count = slot_table.shape[0]
    own = jnp.arange(slot_count, dtype=slot_table.dtype)[:, None]
    full = jnp.concatenate([slot_table[:, :13], own, slot_table[:, 13:]], axis=1)
    full = full.reshape(slot_count, 3, 3, 3)
    reps = np.array([1, extent, 1])
    for axis in (1, 2, 3):
        full = jnp.repeat(full, reps, axis=axis, total_repeat_length=extent + 2)
    return full


def pad_field(wide, sources):
    extent = wide.shape[3]
    tall = jnp.concatenate([wide[:, :, :, extent - 1 :], wide, wide[:, :, :, :1]], axis=3)
    padded = jnp.zeros((sources.shape[0],) + tall.shape[1:], tall.dtype)
    for slot in range(tall.shape[0]):
        padded = jnp.where((sources == slot)[..., None], tall[slot][None], padded)
    return padded


def into_cells(blocks, half_edge):
    slot_count, channels = (blocks.shape[0], blocks.shape[-1])
    lattice = blocks.reshape(slot_count, half_edge, 2, half_edge, 2, half_edge, 2, channels)
    lattice = lattice.transpose(0, 1, 3, 5, 2, 4, 6, 7)
    return lattice.reshape(slot_count * half_edge**3, 8 * channels)


def from_cells(cell_rows, slot_count, half_edge, channels):
    lattice = cell_rows.reshape(slot_count, half_edge, half_edge, half_edge, 2, 2, 2, channels)
    lattice = lattice.transpose(0, 1, 4, 2, 5, 3, 6, 7)
    return lattice.reshape(slot_count, 2 * half_edge, 2 * half_edge, 2 * half_edge, channels)


def conv3(padded, kernel):
    return lax.conv_general_dilated(
        padded,
        kernel,
        (1, 1, 1),
        "VALID",
        dimension_numbers=("NDHWC", "DHWIO", "NDHWC"),
        preferred_element_type=jnp.float32,
    )


def silu_slope(values):
    logistic = jax.nn.sigmoid(values)
    return logistic * (1.0 + values * (1.0 - logistic))


def contract_rows(left, right):
    return lax.dot_general(
        left, right, (((0,), (0,)), ((), ())), preferred_element_type=jnp.float32
    )


def halving(data, axis, dtype):
    me = lax.axis_index(axis)
    size = lax.axis_size(axis)
    data = data.astype(dtype)
    distance = 1
    while distance < size and data.shape[0] > 1:
        bit = (me // distance) % 2
        pairs = data.reshape((data.shape[0] // 2, 2) + data.shape[1:])
        keep = lax.dynamic_index_in_dim(pairs, bit, axis=1, keepdims=False)
        send = lax.dynamic_index_in_dim(pairs, 1 - bit, axis=1, keepdims=False)
        route = [(i, i ^ distance) for i in range(size)]
        data = keep + lax.ppermute(send, axis, route)
        distance *= 2
    return data


def first_bit(data, axis, dtype):
    me = lax.axis_index(axis)
    size = lax.axis_size(axis)
    bit = me % 2
    pairs = data.astype(dtype).reshape((data.shape[0] // 2, 2) + data.shape[1:])
    keep = lax.dynamic_index_in_dim(pairs, bit, axis=1, keepdims=False)
    send = lax.dynamic_index_in_dim(pairs, 1 - bit, axis=1, keepdims=False)
    return keep + lax.ppermute(send, axis, [(i, i ^ 1) for i in range(size)])


def rest_bits(data, axis, dtype, distances):
    me = lax.axis_index(axis)
    size = lax.axis_size(axis)
    data = data.astype(dtype)
    for distance in distances:
        bit = (me // distance) % 2
        pairs = data.reshape((data.shape[0] // 2, 2) + data.shape[1:])
        keep = lax.dynamic_index_in_dim(pairs, bit, axis=1, keepdims=False)
        send = lax.dynamic_index_in_dim(pairs, 1 - bit, axis=1, keepdims=False)
        data = keep + lax.ppermute(send, axis, [(i, i ^ distance) for i in range(size)])
    return data


def reduce_terms(terms):
    blocks = lax.axis_size("gx")
    quarters = lax.axis_size("gy")
    rows = [t.reshape(blocks, -1) for t in terms]
    packed = jnp.concatenate(rows, axis=1)
    width = packed.shape[1]
    packed = first_bit(packed, "gx", jnp.bfloat16)
    bits = (blocks // 2).bit_length() - 1
    grid = packed.reshape((2,) * bits + (quarters, width // quarters))
    order = (bits, bits - 1) + tuple(range(bits - 1)) + (bits + 1,)
    packed = grid.transpose(order).reshape(quarters, blocks // 2, width // quarters)
    part = halving(packed, "gy", jnp.bfloat16)[0]
    distances = [2 ** k for k in range(2, bits + 1)] + [2]
    part = rest_bits(part, "gx", jnp.float32, distances)
    row = lax.all_gather(part, "gy", axis=0, tiled=True).reshape(-1)
    out, start = [], 0
    for t in terms:
        size = t.size // blocks
        piece = row[start : start + size].reshape(t.shape[0] // blocks, t.shape[1], t.shape[2])
        out.append(piece.transpose(1, 0, 2))
        start += size
    return out


def body(features, cotangent, conv_first, down_weight, conv_second, block_count, neighbours):
    inputs = features[0, 0]
    slot_count, extent, channels = (inputs.shape[0], inputs.shape[1], inputs.shape[-1])
    half_edge = extent // 2
    wide_channels = conv_second.shape[-1]
    slot_table = neighbours[0, 0]
    live_mask = (jnp.arange(slot_count) < block_count[0, 0])[:, None, None, None, None]
    inputs = jnp.where(live_mask, inputs, jnp.zeros((), inputs.dtype))
    seed_blocks = jnp.where(live_mask, cotangent[0, 0], jnp.zeros((), inputs.dtype))
    sources_full = source_table(slot_table, extent)
    sources_half = source_table(slot_table, half_edge)

    wide_input, wide_seed = extend_xy([inputs, seed_blocks])
    padded_input = pad_field(wide_input, sources_full)
    first_shape = (3, 3, 3, channels, channels)
    pre_first = conv3(padded_input, conv_first.reshape(first_shape)).reshape(-1, channels)
    hidden_first = jax.nn.silu(pre_first).astype(jnp.bfloat16)
    first_cells = into_cells(
        hidden_first.reshape(slot_count, extent, extent, extent, channels), half_edge
    )
    down_matrix = down_weight.reshape(-1, wide_channels)
    pre_down = jnp.dot(first_cells, down_matrix, preferred_element_type=jnp.float32)
    hidden_down = (
        jax.nn.silu(pre_down)
        .astype(jnp.bfloat16)
        .reshape(slot_count, half_edge, half_edge, half_edge, wide_channels)
    )
    (wide_hidden,) = extend_xy([hidden_down])
    padded_hidden = pad_field(wide_hidden, sources_half)
    kernel_shape = (3, 3, 3, wide_channels, wide_channels)
    output_field = conv3(padded_hidden, conv_second.reshape(kernel_shape)).astype(jnp.bfloat16)
    second_flip = jnp.transpose(conv_second[::-1], (0, 2, 1)).reshape(kernel_shape)
    back_down = conv3(pad_field(wide_seed, sources_half), second_flip).reshape(-1, wide_channels)
    delta_down = (back_down * silu_slope(pre_down)).astype(jnp.bfloat16)
    grad_second = lax.conv_general_dilated(
        padded_hidden,
        seed_blocks,
        (1, 1, 1),
        "VALID",
        dimension_numbers=("CDHWN", "IDHWO", "NDHWC"),
        preferred_element_type=jnp.float32,
    )
    grad_down = contract_rows(first_cells, delta_down)
    back_cells = lax.dot_general(
        delta_down, down_matrix, (((1,), (1,)), ((), ())), preferred_element_type=jnp.float32
    )
    back_first = from_cells(back_cells, slot_count, half_edge, channels).reshape(-1, channels)
    delta_first = (back_first * silu_slope(pre_first)).astype(jnp.bfloat16)
    delta_blocks = delta_first.reshape(slot_count, extent, extent, extent, channels)
    (wide_delta,) = extend_xy([delta_blocks])
    wide_delta, grad_second, grad_down = lax.optimization_barrier((wide_delta, grad_second, grad_down))
    first_flip = jnp.transpose(conv_first[::-1], (0, 2, 1)).reshape(first_shape)
    input_grad = conv3(pad_field(wide_delta, sources_full), first_flip).astype(jnp.bfloat16)
    grad_first = lax.conv_general_dilated(
        padded_input,
        delta_blocks,
        (1, 1, 1),
        "VALID",
        dimension_numbers=("CDHWN", "IDHWO", "NDHWC"),
        preferred_element_type=jnp.float32,
    )
    first_sum, second_sum, down_sum = reduce_terms(
        [
            grad_first.reshape(channels, 27, channels),
            grad_second.reshape(wide_channels, 27, wide_channels),
            grad_down.reshape(8, channels, wide_channels).transpose(1, 0, 2),
        ]
    )
    devices = lax.axis_size("gx") * lax.axis_size("gy")
    scale_first = 1.0 / math.sqrt(float(devices * slot_count * extent**3))
    scale_half = 1.0 / math.sqrt(float(devices * slot_count * half_edge**3))
    return (
        output_field.reshape(1, 1, slot_count, half_edge, half_edge, half_edge, wide_channels),
        input_grad.reshape(1, 1, slot_count, extent, extent, extent, channels),
        first_sum * scale_first,
        down_sum * scale_half,
        second_sum * scale_half,
    )


def solution(mesh):
    placed = (
        P("gx", "gy", None, None, None, None, None),
        P("gx", "gy", None, None, None, None, None),
        P(),
        P(),
        P(),
        P("gx", "gy"),
        P("gx", "gy", None, None),
    )
    return jax.shard_map(
        body,
        mesh=mesh,
        in_specs=placed,
        out_specs=(
            P("gx", "gy", None, None, None, None, None),
            P("gx", "gy", None, None, None, None, None),
            P(None, "gx", None),
            P(None, "gx", None),
            P(None, "gx", None),
        ),
        check_vma=False,
    )
```
